256 devices in a mesh: seq: 32 (over z, x_hi, core), mp: 8 (over x_lo, y).
Axes of the slice: x: 4 (x_hi: 2, x_lo: 2; x = x_hi * 2 + x_lo), y: 4, z: 8, core: 2. Of those that a mesh axis runs over, the one named last changes fastest.
Arguments:
- queries: bfloat16 [4096, 8192], P('seq', 'mp'), may hold values from -200 to 200
- keys: bfloat16 [4096, 1024], P('seq', 'mp'), may hold values from -7 to 7
- values: float32 [4096, 1024], P('seq', 'mp'), may hold values from -24 to 24
- inputs_x: bfloat16 [4096, 8192], P('seq', 'mp'), may hold values from -6 to 6
- in_b: bfloat16 [4096, 128], P('seq'), may hold values from -6 to 6
- in_c: bfloat16 [4096, 128], P('seq'), may hold values from -6 to 6
- log_decay: float32 [4096, 64], P('seq', 'mp'), may hold values from -2 to 0
Outputs:
- grad_x: float32 [4096, 8192], P('seq', 'mp')
- grad_b: float32 [4096, 128], P(('seq', 'mp'))
- grad_c: float32 [4096, 128], P(('seq', 'mp'))
The draws below stay inside these ranges and needn't reach their ends.
All inputs are finite; a program needn't handle non-finite values.
Results may differ from the reference program's by a relative error of at most 0.00035.
Values may be sent and summed in bfloat16 or wider, within the bound.
No kernel may reach another device: no remote copies, remote signals or barrier semaphores. Data moves between devices by JAX's collectives and lax.ppermute only.
A program may use at most 128 MiB of HBM per device.

```python
import math
from functools import partial
import jax
import jax.numpy as jnp
from jax import lax

SHARD_TOKENS = 128
HEAD_WIDTH = 128
N = 128
QUERY_HEADS = 64
KEY_VALUE_HEADS = 8
TOKEN_COUNT = 4096
N_SEQ = 32


def drawn(key):
    base_key_index = jnp.clip(jax.random.normal(jax.random.fold_in(key, 11), (TOKEN_COUNT, KEY_VALUE_HEADS * HEAD_WIDTH), jnp.float32), -6.0, 6.0)
    base_q = 2.0 * jnp.clip(jax.random.normal(jax.random.fold_in(key, 12), (TOKEN_COUNT, QUERY_HEADS * HEAD_WIDTH), jnp.float32), -6.0, 6.0)
    return (base_q, base_key_index)


def draw_queries(key, part):
    return drawn(key)[0].astype(jnp.bfloat16)


def draw_keys(key, part):
    return drawn(key)[1].astype(jnp.bfloat16)


def draw_log_decay(key, part):
    fast_share = 0.5
    fast_heads = jax.random.uniform(jax.random.fold_in(key, 21), (QUERY_HEADS,), jnp.float32) < fast_share
    fast_rate = jax.random.uniform(jax.random.fold_in(key, 22), (QUERY_HEADS,), jnp.float32, 1.0 / 50.0, 1.0 / 30.0)
    slow_total = jnp.exp(jax.random.uniform(jax.random.fold_in(key, 23), (QUERY_HEADS,), jnp.float32, math.log(0.1), math.log(0.3)))
    base_rate = jnp.where(fast_heads, fast_rate, slow_total / TOKEN_COUNT)
    token_factor = jax.random.uniform(jax.random.fold_in(key, 24), (TOKEN_COUNT, QUERY_HEADS), jnp.float32, 0.5, 1.5)
    block_factor = jnp.exp(jax.random.uniform(jax.random.fold_in(key, 25), (TOKEN_COUNT // SHARD_TOKENS, 1, QUERY_HEADS), jnp.float32, math.log(0.5), math.log(2.0)))
    block_factor = jnp.broadcast_to(block_factor, (TOKEN_COUNT // SHARD_TOKENS, SHARD_TOKENS, QUERY_HEADS)).reshape(TOKEN_COUNT, QUERY_HEADS)
    stable_state = -base_rate[None, :] * token_factor * block_factor
    cluster_rows = jax.random.randint(jax.random.fold_in(key, 26), (3, QUERY_HEADS), 0, TOKEN_COUNT)
    cluster_size = jax.random.uniform(jax.random.fold_in(key, 27), (3, QUERY_HEADS), jnp.float32, 0.22, 0.5)
    head_index_list = jnp.broadcast_to(jnp.arange(QUERY_HEADS, dtype=jnp.int32)[None, :], (3, QUERY_HEADS))
    cluster_list = jnp.zeros((TOKEN_COUNT, QUERY_HEADS), jnp.float32).at[cluster_rows, head_index_list].add(-cluster_size)
    return stable_state + cluster_list


def steps_of(key, shape, cuts, low, top_value):
    factor_of, own = 1.0, jax.random.fold_in(key, 6)
    for dim, blocks in cuts:
        draws = jnp.exp(jax.random.uniform(jax.random.fold_in(own, dim), (blocks,), jnp.float32, low / len(cuts), top_value / len(cuts)))
        factor_of = factor_of * jnp.repeat(draws, shape[dim] // blocks).reshape([-1 if axis == dim else 1 for axis in range(len(shape))])
    return factor_of


def normal_values(stream_key, extent, spread, limit, pieces=(), kind=jnp.bfloat16):
    entries = spread * jax.random.normal(stream_key, extent, jnp.float32)
    if pieces:
        entries = entries * steps_of(stream_key, extent, pieces, -0.22, 0.18)
    return jnp.clip(entries, -limit, limit).astype(kind)


def setup_inputs(seed: int = 0) -> dict:
    streams_of = jax.random.split(jax.random.key(seed), 8)
    queries = draw_queries(jax.random.fold_in(streams_of[7], 71), 0)
    keys = draw_keys(jax.random.fold_in(streams_of[7], 71), 0)
    values = normal_values(streams_of[2], (TOKEN_COUNT, KEY_VALUE_HEADS * HEAD_WIDTH), 4.0, 24.0, ((0, 32), (1, 8)), jnp.float32)
    inputs_x = normal_values(streams_of[3], (TOKEN_COUNT, QUERY_HEADS * HEAD_WIDTH), 1.0, 6.0, ((0, 32), (1, 8)))
    in_b = normal_values(streams_of[4], (TOKEN_COUNT, N), 1.0, 6.0, ((0, 32),))
    in_c = normal_values(streams_of[5], (TOKEN_COUNT, N), 1.0, 6.0, ((0, 32),))
    log_decay = draw_log_decay(jax.random.fold_in(streams_of[7], 71), 0)
    return dict(queries=queries, keys=keys, values=values, inputs_x=inputs_x, in_b=in_b, in_c=in_c, log_decay=log_decay)


very_negative = -1e+30
highest = lax.Precision.HIGHEST

def teacher_block(block_data, every_key, every_value):
    query_tile_block, block_start = block_data
    group_width = QUERY_HEADS // KEY_VALUE_HEADS
    query_head_rows = query_tile_block.reshape(SHARD_TOKENS, KEY_VALUE_HEADS, group_width, HEAD_WIDTH).astype(jnp.float32)
    key_head_rows = every_key.reshape(TOKEN_COUNT, KEY_VALUE_HEADS, HEAD_WIDTH).astype(jnp.float32)
    value_head_rows = every_value.reshape(TOKEN_COUNT, KEY_VALUE_HEADS, HEAD_WIDTH).astype(jnp.float32)
    scores = jnp.einsum('qkgd,nkd->qkgn', query_head_rows, key_head_rows, precision=highest) / math.sqrt(HEAD_WIDTH)
    query_pos = block_start + jnp.arange(SHARD_TOKENS, dtype=jnp.int32)
    key_pos = jnp.arange(TOKEN_COUNT, dtype=jnp.int32)
    allowed = (key_pos[None, :] <= query_pos[:, None])[:, None, None, :]
    scores = jnp.where(allowed, scores, very_negative)
    row_top = lax.optimization_barrier(jnp.max(scores, axis=-1, keepdims=True))
    weights = jnp.where(allowed, jnp.exp(scores - row_top), 0.0)
    denominator = lax.optimization_barrier(jnp.sum(weights, axis=-1))
    mixture = jnp.einsum('qkgn,nkd->qkgd', weights, value_head_rows, precision=highest)
    return (mixture / denominator[..., None]).reshape(SHARD_TOKENS, QUERY_HEADS, HEAD_WIDTH)

def decay_matrix(cumulative):
    heads_first = cumulative.T
    causal = jnp.arange(SHARD_TOKENS)[:, None] >= jnp.arange(SHARD_TOKENS)[None, :]
    log_gaps = jnp.where(causal[None], heads_first[:, :, None] - heads_first[:, None, :], -jnp.inf)
    return jnp.exp(log_gaps)

def span_forward(state_in, span_data):
    student_x, b_rows, c_rows, step_logs = span_data
    cumulative = jnp.cumsum(step_logs, axis=0)
    totals = cumulative[-1]
    decays = decay_matrix(cumulative)
    inner_products = jnp.dot(c_rows, b_rows.T, precision=highest)
    mixing = decays * inner_products[None]
    y_intra = jnp.einsum('hts,shp->thp', mixing, student_x, precision=highest)
    rising = jnp.exp(cumulative)
    y_inter = jnp.einsum('tn,hpn->thp', c_rows, state_in, precision=highest) * rising[:, :, None]
    ending = jnp.exp(totals[None, :] - cumulative)
    local_state = jnp.einsum('shp,sn->hpn', student_x * ending[:, :, None], b_rows, precision=highest)
    state_out = jnp.exp(totals)[:, None, None] * state_in + local_state
    return (state_out, (y_intra + y_inter, state_in))

def span_backward(later_grad, span_data):
    student_x, b_rows, c_rows, step_logs, mismatch, state_in = span_data
    cumulative = jnp.cumsum(step_logs, axis=0)
    totals = cumulative[-1]
    decays = decay_matrix(cumulative)
    inner_products = jnp.dot(c_rows, b_rows.T, precision=highest)
    mixing = decays * inner_products[None]
    rising = jnp.exp(cumulative)
    ending = jnp.exp(totals[None, :] - cumulative)
    grad_x = jnp.einsum('hts,thp->shp', mixing, mismatch, precision=highest)
    grad_x = grad_x + jnp.einsum('hpn,sn->shp', later_grad, b_rows, precision=highest) * ending[:, :, None]
    products = jnp.einsum('thp,shp->hts', mismatch, student_x, precision=highest)
    weighted = decays * products
    grad_b = jnp.einsum('hts,tn->sn', weighted, c_rows, precision=highest)
    grad_b = grad_b + jnp.einsum('shp,hpn->sn', student_x * ending[:, :, None], later_grad, precision=highest)
    grad_c = jnp.einsum('hts,sn->tn', weighted, b_rows, precision=highest)
    grad_c = grad_c + jnp.einsum('thp,hpn->tn', mismatch * rising[:, :, None], state_in, precision=highest)
    local_grad = jnp.einsum('thp,tn->hpn', mismatch * rising[:, :, None], c_rows, precision=highest)
    earlier_grad = local_grad + jnp.exp(totals)[:, None, None] * later_grad
    return (earlier_grad, (grad_x, grad_b, grad_c))

def reference(queries, keys, values, inputs_x, in_b, in_c, log_decay):
    starts = jnp.arange(N_SEQ, dtype=jnp.int32) * SHARD_TOKENS
    teacher_out = lax.map(partial(teacher_block, every_key=keys, every_value=values), (queries.reshape(N_SEQ, SHARD_TOKENS, QUERY_HEADS * HEAD_WIDTH), starts))
    c_scale = 0.5 / math.sqrt(N * TOKEN_COUNT)
    student_x = inputs_x.astype(jnp.float32).reshape(N_SEQ, SHARD_TOKENS, QUERY_HEADS, HEAD_WIDTH)
    b_rows = in_b.astype(jnp.float32).reshape(N_SEQ, SHARD_TOKENS, N)
    c_rows = (in_c.astype(jnp.float32) * c_scale).reshape(N_SEQ, SHARD_TOKENS, N)
    step_logs = log_decay.reshape(N_SEQ, SHARD_TOKENS, QUERY_HEADS)
    start_state = jnp.zeros((QUERY_HEADS, HEAD_WIDTH, N), jnp.float32)
    unused_state, (student_out, states_in) = lax.scan(span_forward, start_state, (student_x, b_rows, c_rows, step_logs))
    mismatch = student_out - teacher_out
    unused_grad, (grad_x, grad_b, grad_c) = lax.scan(span_backward, start_state, (student_x, b_rows, c_rows, step_logs, mismatch, states_in), reverse=True)
    return (grad_x.reshape(TOKEN_COUNT, QUERY_HEADS * HEAD_WIDTH), grad_b.reshape(TOKEN_COUNT, N), grad_c.reshape(TOKEN_COUNT, N) * c_scale)
```

```python
import math

import jax
import jax.numpy as jnp
from jax import lax
from jax.sharding import PartitionSpec as P

HEAD_WIDTH = 128
N = 128

very_negative = -1e30
highest = lax.Precision.HIGHEST


def shift(value, axis, distance, forward):
    count = lax.axis_size(axis)
    if forward:
        perm = [(j, j + distance) for j in range(count - distance)]
    else:
        perm = [(j + distance, j) for j in range(count - distance)]
    return lax.ppermute(value, axis, perm)


def exclusive_scan(state, logs, axis, forward):
    count = lax.axis_size(axis)
    window_state, window_log = shift((state, logs), axis, 1, forward)
    width = 1
    while width < count:
        if width * 2 < count:
            got_state, got_log = shift((window_state, window_log), axis, width, forward)
            window_log_next = window_log + got_log
        else:
            got_state = shift(window_state, axis, width, forward)
            window_log_next = window_log
        window_state = window_state + jnp.exp(window_log)[:, None, None] * got_state
        window_log = window_log_next
        width *= 2
    return window_state


def split_bf16(value):
    upper = lax.reduce_precision(value, exponent_bits=8, mantissa_bits=7)
    return upper.astype(jnp.bfloat16), (value - upper).astype(jnp.bfloat16)


def mp_reduce_scatter(value, axis):
    count = lax.axis_size(axis)
    mine = lax.axis_index(axis)
    current = value
    step = count // 2
    while step >= 1:
        half = current.shape[0] // 2
        upper = (mine // step) % 2 == 1
        low_part, high_part = current[:half], current[half:]
        keep = jnp.where(upper, high_part, low_part)
        send = jnp.where(upper, low_part, high_part)
        got = lax.ppermute(send, axis, [(j, j ^ step) for j in range(count)])
        current = keep + got
        step //= 2
    return current


def local(queries, keys, values, inputs_x, in_b, in_c, log_decay):
    row_count = queries.shape[0]
    heads = queries.shape[1] // HEAD_WIDTH
    seq_count = lax.axis_size("seq")
    own_index = lax.axis_index("seq")
    first_query = own_index * row_count

    values_hi, values_lo = split_bf16(values)
    packed = jnp.concatenate([keys, values_hi, values_lo], axis=1)
    every = lax.all_gather(packed, "seq", axis=0, tiled=True)
    every_key = every[:, :HEAD_WIDTH]
    every_hi = every[:, HEAD_WIDTH:2 * HEAD_WIDTH]
    every_lo = every[:, 2 * HEAD_WIDTH:]

    c_scale = 0.5 / math.sqrt(N * row_count * seq_count)
    student_x = inputs_x.astype(jnp.float32).reshape(row_count, heads, HEAD_WIDTH)
    b_rows = in_b.astype(jnp.float32)
    c_rows = in_c.astype(jnp.float32) * c_scale
    cumulative = jnp.cumsum(log_decay, axis=0)
    totals = cumulative[-1]
    heads_first = cumulative.T
    causal = jnp.arange(row_count)[:, None] >= jnp.arange(row_count)[None, :]
    decays = jnp.exp(
        jnp.where(causal[None], heads_first[:, :, None] - heads_first[:, None, :], -jnp.inf)
    )
    inner_products = jnp.dot(in_c, in_b.T, preferred_element_type=jnp.float32) * c_scale
    mixing = decays * inner_products[None]
    rising = jnp.exp(cumulative)
    ending = jnp.exp(totals[None, :] - cumulative)
    local_state = jnp.einsum(
        "shp,sn->hpn", student_x * ending[:, :, None], b_rows, precision=highest
    )
    state_in = exclusive_scan(local_state, totals, "seq", True)

    query_rows = queries.reshape(row_count, heads, HEAD_WIDTH)
    scores = jnp.einsum(
        "qgd,nd->qgn", query_rows, every_key, preferred_element_type=jnp.float32
    ) / math.sqrt(HEAD_WIDTH)
    query_pos = first_query + jnp.arange(row_count, dtype=jnp.int32)
    key_pos = jnp.arange(every.shape[0], dtype=jnp.int32)
    allowed = (key_pos[None, :] <= query_pos[:, None])[:, None, :]
    scores = jnp.where(allowed, scores, very_negative)
    row_top = jnp.max(scores, axis=-1, keepdims=True)
    weights = jnp.where(allowed, jnp.exp(scores - row_top), 0.0)
    denominator = jnp.sum(weights, axis=-1)
    weights_hi, weights_lo = split_bf16(weights)
    mixture = (
        jnp.einsum("qgn,nd->qgd", weights_hi, every_hi, preferred_element_type=jnp.float32)
        + jnp.einsum("qgn,nd->qgd", weights_hi, every_lo, preferred_element_type=jnp.float32)
        + jnp.einsum("qgn,nd->qgd", weights_lo, every_hi, preferred_element_type=jnp.float32)
    )
    teacher_out = mixture / denominator[..., None]

    y_intra = jnp.einsum("hts,shp->thp", mixing, student_x, precision=highest)
    y_inter = jnp.einsum("tn,hpn->thp", c_rows, state_in, precision=highest) * rising[:, :, None]
    mismatch = y_intra + y_inter - teacher_out
    scaled_mismatch = mismatch * rising[:, :, None]
    local_grad = jnp.einsum("thp,tn->hpn", scaled_mismatch, c_rows, precision=highest)
    later_grad = exclusive_scan(local_grad, totals, "seq", False)
    grad_x = jnp.einsum("hts,thp->shp", mixing, mismatch, precision=highest)
    grad_x = (
        grad_x
        + jnp.einsum("hpn,sn->shp", later_grad, b_rows, precision=highest) * ending[:, :, None]
    )
    products = jnp.einsum("thp,shp->hts", mismatch, student_x, precision=highest)
    weighted = decays * products
    grad_b = jnp.einsum("hts,tn->sn", weighted, c_rows, precision=highest)
    grad_b = grad_b + jnp.einsum(
        "shp,hpn->sn", student_x * ending[:, :, None], later_grad, precision=highest
    )
    grad_c = jnp.einsum("hts,sn->tn", weighted, b_rows, precision=highest)
    grad_c = grad_c + jnp.einsum("thp,hpn->tn", scaled_mismatch, state_in, precision=highest)
    summed = mp_reduce_scatter(jnp.concatenate([grad_b, grad_c], axis=1), "mp")
    summed_b, summed_c = summed[:, :N], summed[:, N:]
    return (grad_x.reshape(row_count, heads * HEAD_WIDTH), summed_b, summed_c * c_scale)


def solution(mesh):
    in_specs = (
        P("seq", "mp"),
        P("seq", "mp"),
        P("seq", "mp"),
        P("seq", "mp"),
        P("seq", None),
        P("seq", None),
        P("seq", "mp"),
    )
    out_specs = (P("seq", "mp"), P(("seq", "mp"), None), P(("seq", "mp"), None))
    return jax.shard_map(local, mesh=mesh, in_specs=in_specs, out_specs=out_specs, check_vma=False)
```

```python
import math

import jax
import jax.numpy as jnp
from jax import lax
from jax.sharding import PartitionSpec as P

HEAD_WIDTH = 128
N = 128

very_negative = -1e30
highest = lax.Precision.HIGHEST


def shift(value, axis, distance, forward):
    count = lax.axis_size(axis)
    if forward:
        perm = [(j, j + distance) for j in range(count - distance)]
    else:
        perm = [(j + distance, j) for j in range(count - distance)]
    return lax.ppermute(value, axis, perm)


def exclusive_scan(state, logs, axis, forward):
    count = lax.axis_size(axis)
    chips = count // 2
    core = lax.axis_index(axis) % 2
    first = core == 0 if forward else core == 1
    heads = state.shape[0]
    half = heads // 2
    mine = core * half
    partner = (1 - core) * half
    swap = [(j, j ^ 1) for j in range(count)]

    own_half = lax.dynamic_slice_in_dim(state, mine, half, axis=0)
    got_half, got_logs = lax.ppermute(
        (lax.dynamic_slice_in_dim(state, partner, half, axis=0), logs), axis, swap
    )
    first_half = jnp.where(first, own_half, got_half)
    second_half = jnp.where(first, got_half, own_half)
    first_logs = jnp.where(first, logs, got_logs)
    second_logs = jnp.where(first, got_logs, logs)
    first_logs_half = lax.dynamic_slice_in_dim(first_logs, mine, half)
    second_logs_half = lax.dynamic_slice_in_dim(second_logs, mine, half)
    chip_state = jnp.exp(second_logs_half)[:, None, None] * first_half + second_half
    chip_logs = first_logs_half + second_logs_half

    window_state, window_log = shift((chip_state, chip_logs), axis, 2, forward)
    width = 1
    while width < chips:
        if width * 2 < chips:
            got_state, got_log = shift((window_state, window_log), axis, 2 * width, forward)
            window_log_next = window_log + got_log
        else:
            got_state = shift(window_state, axis, 2 * width, forward)
            window_log_next = window_log
        window_state = window_state + jnp.exp(window_log)[:, None, None] * got_state
        window_log = window_log_next
        width *= 2

    second_state = jnp.exp(first_logs_half)[:, None, None] * window_state + first_half
    keep = jnp.where(first, window_state, second_state)
    send = jnp.where(first, second_state, window_state)
    got = lax.ppermute(send, axis, swap)
    return jnp.where(
        core == 0, jnp.concatenate([keep, got], axis=0), jnp.concatenate([got, keep], axis=0)
    )


def split_bf16(value):
    upper = lax.reduce_precision(value, exponent_bits=8, mantissa_bits=7)
    return upper.astype(jnp.bfloat16), (value - upper).astype(jnp.bfloat16)


def mp_reduce_scatter(value, axis):
    count = lax.axis_size(axis)
    mine = lax.axis_index(axis)
    current = value
    step = count // 2
    while step >= 1:
        half = current.shape[0] // 2
        upper = (mine // step) % 2 == 1
        low_part, high_part = current[:half], current[half:]
        keep = jnp.where(upper, high_part, low_part)
        send = jnp.where(upper, low_part, high_part)
        got = lax.ppermute(send, axis, [(j, j ^ step) for j in range(count)])
        current = keep + got
        step //= 2
    return current


def local(queries, keys, values, inputs_x, in_b, in_c, log_decay):
    row_count = queries.shape[0]
    heads = queries.shape[1] // HEAD_WIDTH
    seq_count = lax.axis_size("seq")
    own_index = lax.axis_index("seq")
    first_query = own_index * row_count

    values_hi, values_lo = split_bf16(values)
    packed = jnp.concatenate([keys, values_hi, values_lo], axis=1)
    every = lax.all_gather(packed, "seq", axis=0, tiled=True)
    every_key = every[:, :HEAD_WIDTH]
    every_hi = every[:, HEAD_WIDTH:2 * HEAD_WIDTH]
    every_lo = every[:, 2 * HEAD_WIDTH:]

    c_scale = 0.5 / math.sqrt(N * row_count * seq_count)
    student_x = inputs_x.astype(jnp.float32).reshape(row_count, heads, HEAD_WIDTH)
    b_rows = in_b.astype(jnp.float32)
    c_rows = in_c.astype(jnp.float32) * c_scale
    cumulative = jnp.cumsum(log_decay, axis=0)
    totals = cumulative[-1]
    heads_first = cumulative.T
    causal = jnp.arange(row_count)[:, None] >= jnp.arange(row_count)[None, :]
    decays = jnp.exp(
        jnp.where(causal[None], heads_first[:, :, None] - heads_first[:, None, :], -jnp.inf)
    )
    inner_products = jnp.dot(in_c, in_b.T, preferred_element_type=jnp.float32) * c_scale
    mixing = decays * inner_products[None]
    rising = jnp.exp(cumulative)
    ending = jnp.exp(totals[None, :] - cumulative)
    local_state = jnp.einsum(
        "shp,sn->hpn", student_x * ending[:, :, None], b_rows, precision=highest
    )
    state_in = exclusive_scan(local_state, totals, "seq", True)

    query_rows = queries.reshape(row_count, heads, HEAD_WIDTH)
    scores = jnp.einsum(
        "qgd,nd->qgn", query_rows, every_key, preferred_element_type=jnp.float32
    ) / math.sqrt(HEAD_WIDTH)
    query_pos = first_query + jnp.arange(row_count, dtype=jnp.int32)
    key_pos = jnp.arange(every.shape[0], dtype=jnp.int32)
    allowed = (key_pos[None, :] <= query_pos[:, None])[:, None, :]
    scores = jnp.where(allowed, scores, very_negative)
    row_top = jnp.max(scores, axis=-1, keepdims=True)
    weights = jnp.where(allowed, jnp.exp(scores - row_top), 0.0)
    denominator = jnp.sum(weights, axis=-1)
    weights_hi, weights_lo = split_bf16(weights)
    mixture = (
        jnp.einsum("qgn,nd->qgd", weights_hi, every_hi, preferred_element_type=jnp.float32)
        + jnp.einsum("qgn,nd->qgd", weights_hi, every_lo, preferred_element_type=jnp.float32)
        + jnp.einsum("qgn,nd->qgd", weights_lo, every_hi, preferred_element_type=jnp.float32)
    )
    teacher_out = mixture / denominator[..., None]

    y_intra = jnp.einsum("hts,shp->thp", mixing, student_x, precision=highest)
    y_inter = jnp.einsum("tn,hpn->thp", c_rows, state_in, precision=highest) * rising[:, :, None]
    mismatch = y_intra + y_inter - teacher_out
    scaled_mismatch = mismatch * rising[:, :, None]
    local_grad = jnp.einsum("thp,tn->hpn", scaled_mismatch, c_rows, precision=highest)
    later_grad = exclusive_scan(local_grad, totals, "seq", False)
    grad_x = jnp.einsum("hts,thp->shp", mixing, mismatch, precision=highest)
    grad_x = (
        grad_x
        + jnp.einsum("hpn,sn->shp", later_grad, b_rows, precision=highest) * ending[:, :, None]
    )
    products = jnp.einsum("thp,shp->hts", mismatch, student_x, precision=highest)
    weighted = decays * products
    grad_b = jnp.einsum("hts,tn->sn", weighted, c_rows, precision=highest)
    grad_b = grad_b + jnp.einsum(
        "shp,hpn->sn", student_x * ending[:, :, None], later_grad, precision=highest
    )
    grad_c = jnp.einsum("hts,sn->tn", weighted, b_rows, precision=highest)
    grad_c = grad_c + jnp.einsum("thp,hpn->tn", scaled_mismatch, state_in, precision=highest)
    summed = mp_reduce_scatter(jnp.concatenate([grad_b, grad_c], axis=1), "mp")
    summed_b, summed_c = summed[:, :N], summed[:, N:]
    return (grad_x.reshape(row_count, heads * HEAD_WIDTH), summed_b, summed_c * c_scale)


def solution(mesh):
    in_specs = (
        P("seq", "mp"),
        P("seq", "mp"),
        P("seq", "mp"),
        P("seq", "mp"),
        P("seq", None),
        P("seq", None),
        P("seq", "mp"),
    )
    out_specs = (P("seq", "mp"), P(("seq", "mp"), None), P(("seq", "mp"), None))
    return jax.shard_map(local, mesh=mesh, in_specs=in_specs, out_specs=out_specs, check_vma=False)
```

```python
import math

import jax
import jax.numpy as jnp
from jax import lax
from jax.sharding import PartitionSpec as P

HEAD_WIDTH = 128
N = 128

very_negative = -1e30
highest = lax.Precision.HIGHEST


def shift(value, axis, distance, forward):
    count = lax.axis_size(axis)
    if forward:
        perm = [(j, j + distance) for j in range(count - distance)]
    else:
        perm = [(j + distance, j) for j in range(count - distance)]
    return lax.ppermute(value, axis, perm)


def exclusive_scan(state, logs, axis, forward):
    count = lax.axis_size(axis)
    chips = count // 2
    core = lax.axis_index(axis) % 2
    first = core == 0 if forward else core == 1
    heads = state.shape[0]
    half = heads // 2
    mine = core * half
    partner = (1 - core) * half
    swap = [(j, j ^ 1) for j in range(count)]

    own_half = lax.dynamic_slice_in_dim(state, mine, half, axis=0)
    got_half, got_logs = lax.ppermute(
        (lax.dynamic_slice_in_dim(state, partner, half, axis=0), logs), axis, swap
    )
    first_half = jnp.where(first, own_half, got_half)
    second_half = jnp.where(first, got_half, own_half)
    first_logs = jnp.where(first, logs, got_logs)
    second_logs = jnp.where(first, got_logs, logs)
    first_logs_half = lax.dynamic_slice_in_dim(first_logs, mine, half)
    second_logs_half = lax.dynamic_slice_in_dim(second_logs, mine, half)
    chip_state = jnp.exp(second_logs_half)[:, None, None] * first_half + second_half
    chip_logs = first_logs_half + second_logs_half

    window_state, window_log = shift((chip_state, chip_logs), axis, 2, forward)
    width = 1
    while width < chips:
        if width * 2 < chips:
            got_state, got_log = shift((window_state, window_log), axis, 2 * width, forward)
            window_log_next = window_log + got_log
        else:
            got_state = shift(window_state, axis, 2 * width, forward)
            window_log_next = window_log
        window_state = window_state + jnp.exp(window_log)[:, None, None] * got_state
        window_log = window_log_next
        width *= 2

    second_state = jnp.exp(first_logs_half)[:, None, None] * window_state + first_half
    keep = jnp.where(first, window_state, second_state)
    send = jnp.where(first, second_state, window_state)
    got = lax.ppermute(send, axis, swap)
    return jnp.where(
        core == 0, jnp.concatenate([keep, got], axis=0), jnp.concatenate([got, keep], axis=0)
    )


def split_bf16(value):
    upper = lax.reduce_precision(value, exponent_bits=8, mantissa_bits=7)
    return upper.astype(jnp.bfloat16), (value - upper).astype(jnp.bfloat16)


def mp_sum_scatter(value, axis):
    count = lax.axis_size(axis)
    blocks = value.reshape(count, value.shape[0] // count, value.shape[1])
    return jnp.sum(lax.all_to_all(blocks, axis, 0, 0), axis=0)


def local(queries, keys, values, inputs_x, in_b, in_c, log_decay):
    row_count = queries.shape[0]
    heads = queries.shape[1] // HEAD_WIDTH
    seq_count = lax.axis_size("seq")
    own_index = lax.axis_index("seq")
    first_query = own_index * row_count

    values_hi, values_lo = split_bf16(values)
    packed = jnp.concatenate([keys, values_hi, values_lo], axis=1)
    every = lax.all_gather(packed, "seq", axis=0, tiled=True)
    every_key = every[:, :HEAD_WIDTH]
    every_hi = every[:, HEAD_WIDTH:2 * HEAD_WIDTH]
    every_lo = every[:, 2 * HEAD_WIDTH:]

    c_scale = 0.5 / math.sqrt(N * row_count * seq_count)
    student_x = inputs_x.astype(jnp.float32).reshape(row_count, heads, HEAD_WIDTH)
    b_rows = in_b.astype(jnp.float32)
    c_rows = in_c.astype(jnp.float32) * c_scale
    cumulative = jnp.cumsum(log_decay, axis=0)
    totals = cumulative[-1]
    heads_first = cumulative.T
    causal = jnp.arange(row_count)[:, None] >= jnp.arange(row_count)[None, :]
    decays = jnp.exp(
        jnp.where(causal[None], heads_first[:, :, None] - heads_first[:, None, :], -jnp.inf)
    )
    inner_products = jnp.dot(in_c, in_b.T, preferred_element_type=jnp.float32) * c_scale
    mixing = decays * inner_products[None]
    rising = jnp.exp(cumulative)
    ending = jnp.exp(totals[None, :] - cumulative)
    local_state = jnp.einsum(
        "shp,sn->hpn", student_x * ending[:, :, None], b_rows, precision=highest
    )
    state_in = exclusive_scan(local_state, totals, "seq", True)

    query_rows = queries.reshape(row_count, heads, HEAD_WIDTH)
    scores = jnp.einsum(
        "qgd,nd->qgn", query_rows, every_key, preferred_element_type=jnp.float32
    ) / math.sqrt(HEAD_WIDTH)
    query_pos = first_query + jnp.arange(row_count, dtype=jnp.int32)
    key_pos = jnp.arange(every.shape[0], dtype=jnp.int32)
    allowed = (key_pos[None, :] <= query_pos[:, None])[:, None, :]
    scores = jnp.where(allowed, scores, very_negative)
    row_top = jnp.max(scores, axis=-1, keepdims=True)
    weights = jnp.where(allowed, jnp.exp(scores - row_top), 0.0)
    denominator = jnp.sum(weights, axis=-1)
    weights_hi, weights_lo = split_bf16(weights)
    mixture = (
        jnp.einsum("qgn,nd->qgd", weights_hi, every_hi, preferred_element_type=jnp.float32)
        + jnp.einsum("qgn,nd->qgd", weights_hi, every_lo, preferred_element_type=jnp.float32)
        + jnp.einsum("qgn,nd->qgd", weights_lo, every_hi, preferred_element_type=jnp.float32)
    )
    teacher_out = mixture / denominator[..., None]

    y_intra = jnp.einsum("hts,shp->thp", mixing, student_x, precision=highest)
    y_inter = jnp.einsum("tn,hpn->thp", c_rows, state_in, precision=highest) * rising[:, :, None]
    mismatch = y_intra + y_inter - teacher_out
    scaled_mismatch = mismatch * rising[:, :, None]
    local_grad = jnp.einsum("thp,tn->hpn", scaled_mismatch, c_rows, precision=highest)
    later_grad = exclusive_scan(local_grad, totals, "seq", False)
    grad_x = jnp.einsum("hts,thp->shp", mixing, mismatch, precision=highest)
    grad_x = (
        grad_x
        + jnp.einsum("hpn,sn->shp", later_grad, b_rows, precision=highest) * ending[:, :, None]
    )
    products = jnp.einsum("thp,shp->hts", mismatch, student_x, precision=highest)
    weighted = decays * products
    grad_b = jnp.einsum("hts,tn->sn", weighted, c_rows, precision=highest)
    grad_c = jnp.einsum("hts,sn->tn", weighted, b_rows, precision=highest)
    grad_c = grad_c + jnp.einsum("thp,hpn->tn", scaled_mismatch, state_in, precision=highest)
    early = mp_sum_scatter(jnp.concatenate([grad_b, grad_c], axis=1), "mp")
    grad_b_later = jnp.einsum(
        "shp,hpn->sn", student_x * ending[:, :, None], later_grad, precision=highest
    )
    summed_b = early[:, :N] + mp_sum_scatter(grad_b_later, "mp")
    summed_c = early[:, N:]
    return (grad_x.reshape(row_count, heads * HEAD_WIDTH), summed_b, summed_c * c_scale)


def solution(mesh):
    in_specs = (
        P("seq", "mp"),
        P("seq", "mp"),
        P("seq", "mp"),
        P("seq", "mp"),
        P("seq", None),
        P("seq", None),
        P("seq", "mp"),
    )
    out_specs = (P("seq", "mp"), P(("seq", "mp"), None), P(("seq", "mp"), None))
    return jax.shard_map(local, mesh=mesh, in_specs=in_specs, out_specs=out_specs, check_vma=False)
```

```python
import functools
import math

import jax
import jax.numpy as jnp
from jax import lax
from jax.experimental import pallas as pl
from jax.experimental.pallas import tpu as pltpu
from jax.sharding import PartitionSpec as P

HEAD_WIDTH = 128
N = 128

very_negative = -1e30
highest = lax.Precision.HIGHEST


def shift(value, axis, distance, forward):
    count = lax.axis_size(axis)
    if forward:
        perm = [(j, j + distance) for j in range(count - distance)]
    else:
        perm = [(j + distance, j) for j in range(count - distance)]
    return lax.ppermute(value, axis, perm)


def exclusive_scan(state, logs, axis, forward):
    count = lax.axis_size(axis)
    chips = count // 2
    core = lax.axis_index(axis) % 2
    first = core == 0 if forward else core == 1
    heads = state.shape[0]
    half = heads // 2
    mine = core * half
    partner = (1 - core) * half
    swap = [(j, j ^ 1) for j in range(count)]

    own_half = lax.dynamic_slice_in_dim(state, mine, half, axis=0)
    got_half, got_logs = lax.ppermute(
        (lax.dynamic_slice_in_dim(state, partner, half, axis=0), logs), axis, swap
    )
    first_half = jnp.where(first, own_half, got_half)
    second_half = jnp.where(first, got_half, own_half)
    first_logs = jnp.where(first, logs, got_logs)
    second_logs = jnp.where(first, got_logs, logs)
    first_logs_half = lax.dynamic_slice_in_dim(first_logs, mine, half)
    second_logs_half = lax.dynamic_slice_in_dim(second_logs, mine, half)
    chip_state = jnp.exp(second_logs_half)[:, None, None] * first_half + second_half
    chip_logs = first_logs_half + second_logs_half

    window_state, window_log = shift((chip_state, chip_logs), axis, 2, forward)
    width = 1
    while width < chips:
        if width * 2 < chips:
            got_state, got_log = shift((window_state, window_log), axis, 2 * width, forward)
            window_log_next = window_log + got_log
        else:
            got_state = shift(window_state, axis, 2 * width, forward)
            window_log_next = window_log
        window_state = window_state + jnp.exp(window_log)[:, None, None] * got_state
        window_log = window_log_next
        width *= 2

    second_state = jnp.exp(first_logs_half)[:, None, None] * window_state + first_half
    keep = jnp.where(first, window_state, second_state)
    send = jnp.where(first, second_state, window_state)
    got = lax.ppermute(send, axis, swap)
    return jnp.where(
        core == 0, jnp.concatenate([keep, got], axis=0), jnp.concatenate([got, keep], axis=0)
    )


def split_bf16(value):
    upper = lax.reduce_precision(value, exponent_bits=8, mantissa_bits=7)
    return upper.astype(jnp.bfloat16), (value - upper).astype(jnp.bfloat16)


def mp_sum_scatter(value, axis):
    count = lax.axis_size(axis)
    blocks = value.reshape(count, value.shape[0] // count, value.shape[1])
    return jnp.sum(lax.all_to_all(blocks, axis, 0, 0), axis=0)


def attend_kernel(first_ref, query_ref, key_ref, upper_ref, lower_ref, out_ref, top_ref, total_ref, mix_ref, *, heads):
    block = pl.program_id(0)
    rows = query_ref.shape[0]
    width = query_ref.shape[1]
    keys_per_block = key_ref.shape[0]
    first = first_ref[0]

    @pl.when(block == 0)
    def _():
        top_ref[...] = jnp.full(top_ref.shape, very_negative, jnp.float32)
        total_ref[...] = jnp.zeros(total_ref.shape, jnp.float32)
        mix_ref[...] = jnp.zeros(mix_ref.shape, jnp.float32)

    @pl.when(block * keys_per_block <= first + rows // heads - 1)
    def _():
        scores = lax.dot_general(
            query_ref[...], key_ref[...], (((1,), (1,)), ((), ())), preferred_element_type=jnp.float32
        ) / math.sqrt(width)
        row = lax.broadcasted_iota(jnp.int32, scores.shape, 0)
        col = lax.broadcasted_iota(jnp.int32, scores.shape, 1)
        allowed = block * keys_per_block + col <= first + row // heads
        scores = jnp.where(allowed, scores, very_negative)
        top_old = top_ref[...]
        top_new = jnp.maximum(top_old, jnp.max(scores, axis=1, keepdims=True))
        rescale = jnp.exp(top_old - top_new)
        weights = jnp.where(allowed, jnp.exp(scores - top_new), 0.0)
        total_ref[...] = rescale * total_ref[...] + jnp.sum(weights, axis=1, keepdims=True)
        weights_hi = weights.astype(jnp.bfloat16)
        weights_lo = (weights - weights_hi.astype(jnp.float32)).astype(jnp.bfloat16)
        upper = upper_ref[...]
        mixed = (
            jnp.dot(weights_hi, upper, preferred_element_type=jnp.float32)
            + jnp.dot(weights_hi, lower_ref[...], preferred_element_type=jnp.float32)
            + jnp.dot(weights_lo, upper, preferred_element_type=jnp.float32)
        )
        mix_ref[...] = rescale * mix_ref[...] + mixed
        top_ref[...] = top_new

    @pl.when(block == pl.num_programs(0) - 1)
    def _():
        out_ref[...] = mix_ref[...] / total_ref[...]


def attend(first_query, query_rows, every, heads, keys_per_block=512):
    rows, width = query_rows.shape
    blocks = every.shape[0] // keys_per_block
    flops = 2 * rows * every.shape[0] * width * 4
    return pl.pallas_call(
        functools.partial(attend_kernel, heads=heads),
        out_shape=jax.ShapeDtypeStruct((rows, width), jnp.float32),
        grid_spec=pltpu.PrefetchScalarGridSpec(
            num_scalar_prefetch=1,
            grid=(blocks,),
            in_specs=[
                pl.BlockSpec((rows, width), lambda b, f: (0, 0)),
                pl.BlockSpec((keys_per_block, width), lambda b, f: (b, 0)),
                pl.BlockSpec((keys_per_block, width), lambda b, f: (b, 1)),
                pl.BlockSpec((keys_per_block, width), lambda b, f: (b, 2)),
            ],
            out_specs=pl.BlockSpec((rows, width), lambda b, f: (0, 0)),
            scratch_shapes=[
                pltpu.VMEM((rows, 1), jnp.float32),
                pltpu.VMEM((rows, 1), jnp.float32),
                pltpu.VMEM((rows, width), jnp.float32),
            ],
        ),
        compiler_params=pltpu.CompilerParams(dimension_semantics=("arbitrary",)),
        cost_estimate=pl.CostEstimate(
            flops=flops,
            transcendentals=rows * every.shape[0],
            bytes_accessed=every.size * 2 + query_rows.size * 2 + rows * width * 4,
        ),
    )(first_query, query_rows, every, every, every)


def local(queries, keys, values, inputs_x, in_b, in_c, log_decay):
    row_count = queries.shape[0]
    heads = queries.shape[1] // HEAD_WIDTH
    seq_count = lax.axis_size("seq")
    own_index = lax.axis_index("seq")
    first_query = own_index * row_count

    values_hi, values_lo = split_bf16(values)
    packed = jnp.concatenate([keys, values_hi, values_lo], axis=1)
    every = lax.all_gather(packed, "seq", axis=0, tiled=True)

    c_scale = 0.5 / math.sqrt(N * row_count * seq_count)
    student_x = inputs_x.astype(jnp.float32).reshape(row_count, heads, HEAD_WIDTH)
    b_rows = in_b.astype(jnp.float32)
    c_rows = in_c.astype(jnp.float32) * c_scale
    cumulative = jnp.cumsum(log_decay, axis=0)
    totals = cumulative[-1]
    heads_first = cumulative.T
    causal = jnp.arange(row_count)[:, None] >= jnp.arange(row_count)[None, :]
    decays = jnp.exp(
        jnp.where(causal[None], heads_first[:, :, None] - heads_first[:, None, :], -jnp.inf)
    )
    inner_products = jnp.dot(in_c, in_b.T, preferred_element_type=jnp.float32) * c_scale
    mixing = decays * inner_products[None]
    rising = jnp.exp(cumulative)
    ending = jnp.exp(totals[None, :] - cumulative)
    local_state = jnp.einsum(
        "shp,sn->hpn", student_x * ending[:, :, None], b_rows, precision=highest
    )
    state_in = exclusive_scan(local_state, totals, "seq", True)

    query_rows = queries.reshape(row_count * heads, HEAD_WIDTH)
    teacher_out = attend(
        jnp.reshape(first_query, (1,)).astype(jnp.int32), query_rows, every, heads
    ).reshape(row_count, heads, HEAD_WIDTH)

    y_intra = jnp.einsum("hts,shp->thp", mixing, student_x, precision=highest)
    y_inter = jnp.einsum("tn,hpn->thp", c_rows, state_in, precision=highest) * rising[:, :, None]
    mismatch = y_intra + y_inter - teacher_out
    scaled_mismatch = mismatch * rising[:, :, None]
    local_grad = jnp.einsum("thp,tn->hpn", scaled_mismatch, c_rows, precision=highest)
    later_grad = exclusive_scan(local_grad, totals, "seq", False)
    grad_x = jnp.einsum("hts,thp->shp", mixing, mismatch, precision=highest)
    grad_x = (
        grad_x
        + jnp.einsum("hpn,sn->shp", later_grad, b_rows, precision=highest) * ending[:, :, None]
    )
    products = jnp.einsum("thp,shp->hts", mismatch, student_x, precision=highest)
    weighted = decays * products
    grad_b = jnp.einsum("hts,tn->sn", weighted, c_rows, precision=highest)
    grad_b = grad_b + jnp.einsum(
        "shp,hpn->sn", student_x * ending[:, :, None], later_grad, precision=highest
    )
    grad_c = jnp.einsum("hts,sn->tn", weighted, b_rows, precision=highest)
    grad_c = grad_c + jnp.einsum("thp,hpn->tn", scaled_mismatch, state_in, precision=highest)
    summed = mp_sum_scatter(jnp.concatenate([grad_b, grad_c], axis=1), "mp")
    summed_b, summed_c = summed[:, :N], summed[:, N:]
    return (grad_x.reshape(row_count, heads * HEAD_WIDTH), summed_b, summed_c * c_scale)


def solution(mesh):
    in_specs = (
        P("seq", "mp"),
        P("seq", "mp"),
        P("seq", "mp"),
        P("seq", "mp"),
        P("seq", None),
        P("seq", None),
        P("seq", "mp"),
    )
    out_specs = (P("seq", "mp"), P(("seq", "mp"), None), P(("seq", "mp"), None))
    return jax.shard_map(local, mesh=mesh, in_specs=in_specs, out_specs=out_specs, check_vma=False)
```

```python
import functools
import math

import jax
import jax.numpy as jnp
from jax import lax
from jax.experimental import pallas as pl
from jax.experimental.pallas import tpu as pltpu
from jax.sharding import PartitionSpec as P

HEAD_WIDTH = 128
N = 128

very_negative = -1e30
highest = lax.Precision.HIGHEST


def shift(value, axis, distance, forward):
    count = lax.axis_size(axis)
    if forward:
        perm = [(j, j + distance) for j in range(count - distance)]
    else:
        perm = [(j + distance, j) for j in range(count - distance)]
    return lax.ppermute(value, axis, perm)


def send_with_logs(state, logs, axis, perm):
    heads, rows, width = state.shape
    count = logs.shape[0]
    log_rows = jnp.pad(jnp.broadcast_to(logs[:, None], (count, width)), ((0, -count % 8), (0, 0)))
    payload = jnp.concatenate([state.reshape(heads * rows, width), log_rows], axis=0)
    got = lax.ppermute(payload, axis, perm)
    return got[: heads * rows].reshape(heads, rows, width), got[heads * rows : heads * rows + count, 0]


def shift_perm(count, distance, forward):
    if forward:
        return [(j, j + distance) for j in range(count - distance)]
    return [(j + distance, j) for j in range(count - distance)]


def exclusive_scan(state, logs, axis, forward):
    count = lax.axis_size(axis)
    chips = count // 2
    core = lax.axis_index(axis) % 2
    first = core == 0 if forward else core == 1
    heads = state.shape[0]
    half = heads // 2
    mine = core * half
    partner = (1 - core) * half
    swap = [(j, j ^ 1) for j in range(count)]

    own_half = lax.dynamic_slice_in_dim(state, mine, half, axis=0)
    got_half, got_logs = send_with_logs(
        lax.dynamic_slice_in_dim(state, partner, half, axis=0), logs, axis, swap
    )
    first_half = jnp.where(first, own_half, got_half)
    second_half = jnp.where(first, got_half, own_half)
    first_logs = jnp.where(first, logs, got_logs)
    second_logs = jnp.where(first, got_logs, logs)
    first_logs_half = lax.dynamic_slice_in_dim(first_logs, mine, half)
    second_logs_half = lax.dynamic_slice_in_dim(second_logs, mine, half)
    chip_state = jnp.exp(second_logs_half)[:, None, None] * first_half + second_half
    chip_logs = first_logs_half + second_logs_half

    window_state, window_log = send_with_logs(chip_state, chip_logs, axis, shift_perm(count, 2, forward))
    width = 1
    while width < chips:
        if width * 2 < chips:
            got_state, got_log = send_with_logs(
                window_state, window_log, axis, shift_perm(count, 2 * width, forward)
            )
            window_log_next = window_log + got_log
        else:
            got_state = shift(window_state, axis, 2 * width, forward)
            window_log_next = window_log
        window_state = window_state + jnp.exp(window_log)[:, None, None] * got_state
        window_log = window_log_next
        width *= 2

    second_state = jnp.exp(first_logs_half)[:, None, None] * window_state + first_half
    keep = jnp.where(first, window_state, second_state)
    send = jnp.where(first, second_state, window_state)
    got = lax.ppermute(send, axis, swap)
    return jnp.where(
        core == 0, jnp.concatenate([keep, got], axis=0), jnp.concatenate([got, keep], axis=0)
    )


def split_bf16(value):
    upper = lax.reduce_precision(value, exponent_bits=8, mantissa_bits=7)
    return upper.astype(jnp.bfloat16), (value - upper).astype(jnp.bfloat16)


def mp_sum_scatter(value, axis):
    count = lax.axis_size(axis)
    blocks = value.reshape(count, value.shape[0] // count, value.shape[1])
    return jnp.sum(lax.all_to_all(blocks, axis, 0, 0), axis=0)


def attend_kernel(first_ref, query_ref, key_ref, upper_ref, lower_ref, out_ref, top_ref, total_ref, mix_ref, *, heads):
    block = pl.program_id(0)
    rows = query_ref.shape[0]
    width = query_ref.shape[1]
    keys_per_block = key_ref.shape[0]
    first = first_ref[0]

    @pl.when(block == 0)
    def _():
        top_ref[...] = jnp.full(top_ref.shape, very_negative, jnp.float32)
        total_ref[...] = jnp.zeros(total_ref.shape, jnp.float32)
        mix_ref[...] = jnp.zeros(mix_ref.shape, jnp.float32)

    @pl.when(block * keys_per_block <= first + rows // heads - 1)
    def _():
        scores = lax.dot_general(
            query_ref[...], key_ref[...], (((1,), (1,)), ((), ())), preferred_element_type=jnp.float32
        ) / math.sqrt(width)
        row = lax.broadcasted_iota(jnp.int32, scores.shape, 0)
        col = lax.broadcasted_iota(jnp.int32, scores.shape, 1)
        allowed = block * keys_per_block + col <= first + row // heads
        scores = jnp.where(allowed, scores, very_negative)
        top_old = top_ref[...]
        top_new = jnp.maximum(top_old, jnp.max(scores, axis=1, keepdims=True))
        rescale = jnp.exp(top_old - top_new)
        weights = jnp.where(allowed, jnp.exp(scores - top_new), 0.0)
        total_ref[...] = rescale * total_ref[...] + jnp.sum(weights, axis=1, keepdims=True)
        weights_hi = weights.astype(jnp.bfloat16)
        weights_lo = (weights - weights_hi.astype(jnp.float32)).astype(jnp.bfloat16)
        upper = upper_ref[...]
        mixed = (
            jnp.dot(weights_hi, upper, preferred_element_type=jnp.float32)
            + jnp.dot(weights_hi, lower_ref[...], preferred_element_type=jnp.float32)
            + jnp.dot(weights_lo, upper, preferred_element_type=jnp.float32)
        )
        mix_ref[...] = rescale * mix_ref[...] + mixed
        top_ref[...] = top_new

    @pl.when(block == pl.num_programs(0) - 1)
    def _():
        out_ref[...] = mix_ref[...] / total_ref[...]


def attend(first_query, query_rows, every, heads, keys_per_block=512):
    rows, width = query_rows.shape
    blocks = every.shape[0] // keys_per_block
    flops = 2 * rows * every.shape[0] * width * 4
    return pl.pallas_call(
        functools.partial(attend_kernel, heads=heads),
        out_shape=jax.ShapeDtypeStruct((rows, width), jnp.float32),
        grid_spec=pltpu.PrefetchScalarGridSpec(
            num_scalar_prefetch=1,
            grid=(blocks,),
            in_specs=[
                pl.BlockSpec((rows, width), lambda b, f: (0, 0)),
                pl.BlockSpec((keys_per_block, width), lambda b, f: (b, 0)),
                pl.BlockSpec((keys_per_block, width), lambda b, f: (b, 1)),
                pl.BlockSpec((keys_per_block, width), lambda b, f: (b, 2)),
            ],
            out_specs=pl.BlockSpec((rows, width), lambda b, f: (0, 0)),
            scratch_shapes=[
                pltpu.VMEM((rows, 1), jnp.float32),
                pltpu.VMEM((rows, 1), jnp.float32),
                pltpu.VMEM((rows, width), jnp.float32),
            ],
        ),
        compiler_params=pltpu.CompilerParams(dimension_semantics=("arbitrary",)),
        cost_estimate=pl.CostEstimate(
            flops=flops,
            transcendentals=rows * every.shape[0],
            bytes_accessed=every.size * 2 + query_rows.size * 2 + rows * width * 4,
        ),
    )(first_query, query_rows, every, every, every)


def local(queries, keys, values, inputs_x, in_b, in_c, log_decay):
    row_count = queries.shape[0]
    heads = queries.shape[1] // HEAD_WIDTH
    seq_count = lax.axis_size("seq")
    own_index = lax.axis_index("seq")
    first_query = own_index * row_count

    values_hi, values_lo = split_bf16(values)
    packed = jnp.concatenate([keys, values_hi, values_lo], axis=1)
    every = lax.all_gather(packed, "seq", axis=0, tiled=True)

    c_scale = 0.5 / math.sqrt(N * row_count * seq_count)
    student_x = inputs_x.astype(jnp.float32).reshape(row_count, heads, HEAD_WIDTH)
    b_rows = in_b.astype(jnp.float32)
    c_rows = in_c.astype(jnp.float32) * c_scale
    cumulative = jnp.cumsum(log_decay, axis=0)
    totals = cumulative[-1]
    heads_first = cumulative.T
    causal = jnp.arange(row_count)[:, None] >= jnp.arange(row_count)[None, :]
    decays = jnp.exp(
        jnp.where(causal[None], heads_first[:, :, None] - heads_first[:, None, :], -jnp.inf)
    )
    inner_products = jnp.dot(in_c, in_b.T, preferred_element_type=jnp.float32) * c_scale
    mixing = decays * inner_products[None]
    rising = jnp.exp(cumulative)
    ending = jnp.exp(totals[None, :] - cumulative)
    local_state = jnp.einsum(
        "shp,sn->hpn", student_x * ending[:, :, None], b_rows, precision=highest
    )
    state_in = exclusive_scan(local_state, totals, "seq", True)

    query_rows = queries.reshape(row_count * heads, HEAD_WIDTH)
    teacher_out = attend(
        jnp.reshape(first_query, (1,)).astype(jnp.int32), query_rows, every, heads
    ).reshape(row_count, heads, HEAD_WIDTH)

    y_intra = jnp.einsum("hts,shp->thp", mixing, student_x, precision=highest)
    y_inter = jnp.einsum("tn,hpn->thp", c_rows, state_in, precision=highest) * rising[:, :, None]
    mismatch = y_intra + y_inter - teacher_out
    scaled_mismatch = mismatch * rising[:, :, None]
    local_grad = jnp.einsum("thp,tn->hpn", scaled_mismatch, c_rows, precision=highest)
    later_grad = exclusive_scan(local_grad, totals, "seq", False)
    grad_x = jnp.einsum("hts,thp->shp", mixing, mismatch, precision=highest)
    grad_x = (
        grad_x
        + jnp.einsum("hpn,sn->shp", later_grad, b_rows, precision=highest) * ending[:, :, None]
    )
    products = jnp.einsum("thp,shp->hts", mismatch, student_x, precision=highest)
    weighted = decays * products
    grad_b = jnp.einsum("hts,tn->sn", weighted, c_rows, precision=highest)
    grad_b = grad_b + jnp.einsum(
        "shp,hpn->sn", student_x * ending[:, :, None], later_grad, precision=highest
    )
    grad_c = jnp.einsum("hts,sn->tn", weighted, b_rows, precision=highest)
    grad_c = grad_c + jnp.einsum("thp,hpn->tn", scaled_mismatch, state_in, precision=highest)
    summed = mp_sum_scatter(jnp.concatenate([grad_b, grad_c], axis=1), "mp")
    summed_b, summed_c = summed[:, :N], summed[:, N:]
    return (grad_x.reshape(row_count, heads * HEAD_WIDTH), summed_b, summed_c * c_scale)


def solution(mesh):
    in_specs = (
        P("seq", "mp"),
        P("seq", "mp"),
        P("seq", "mp"),
        P("seq", "mp"),
        P("seq", None),
        P("seq", None),
        P("seq", "mp"),
    )
    out_specs = (P("seq", "mp"), P(("seq", "mp"), None), P(("seq", "mp"), None))
    return jax.shard_map(local, mesh=mesh, in_specs=in_specs, out_specs=out_specs, check_vma=False)
```

```python
import functools
import math

import jax
import jax.numpy as jnp
from jax import lax
from jax.experimental import pallas as pl
from jax.experimental.pallas import tpu as pltpu
from jax.sharding import PartitionSpec as P

HEAD_WIDTH = 128
N = 128

very_negative = -1e30
highest = lax.Precision.HIGHEST


def shift(value, axis, distance, forward):
    count = lax.axis_size(axis)
    if forward:
        perm = [(j, j + distance) for j in range(count - distance)]
    else:
        perm = [(j + distance, j) for j in range(count - distance)]
    return lax.ppermute(value, axis, perm)


def send_with_logs(state, logs, axis, perm):
    heads, rows, width = state.shape
    count = logs.shape[0]
    log_rows = jnp.pad(jnp.broadcast_to(logs[:, None], (count, width)), ((0, -count % 8), (0, 0)))
    payload = jnp.concatenate([state.reshape(heads * rows, width), log_rows], axis=0)
    got = lax.ppermute(payload, axis, perm)
    return got[: heads * rows].reshape(heads, rows, width), got[heads * rows : heads * rows + count, 0]


def shift_perm(count, distance, forward):
    if forward:
        return [(j, j + distance) for j in range(count - distance)]
    return [(j + distance, j) for j in range(count - distance)]


def pair_down(state, logs, axis, bit, forward):
    count = lax.axis_size(axis)
    upper = (lax.axis_index(axis) // bit) % 2 == 1
    first = jnp.logical_not(upper) if forward else upper
    half = state.shape[0] // 2
    mine = jnp.where(upper, half, 0)
    other = half - mine
    own_state = lax.dynamic_slice_in_dim(state, mine, half, axis=0)
    own_logs = lax.dynamic_slice_in_dim(logs, mine, half)
    got_state, got_logs = send_with_logs(
        lax.dynamic_slice_in_dim(state, other, half, axis=0),
        lax.dynamic_slice_in_dim(logs, other, half),
        axis,
        [(j, j ^ bit) for j in range(count)],
    )
    first_state = jnp.where(first, own_state, got_state)
    second_state = jnp.where(first, got_state, own_state)
    first_logs = jnp.where(first, own_logs, got_logs)
    second_logs = jnp.where(first, got_logs, own_logs)
    pair_state = jnp.exp(second_logs)[:, None, None] * first_state + second_state
    return pair_state, first_logs + second_logs, (first_state, first_logs)


def pair_up(window, saved, axis, bit, forward):
    count = lax.axis_size(axis)
    upper = (lax.axis_index(axis) // bit) % 2 == 1
    first = jnp.logical_not(upper) if forward else upper
    first_state, first_logs = saved
    second_window = jnp.exp(first_logs)[:, None, None] * window + first_state
    keep = jnp.where(first, window, second_window)
    send = jnp.where(first, second_window, window)
    got = lax.ppermute(send, axis, [(j, j ^ bit) for j in range(count)])
    return jnp.where(
        upper, jnp.concatenate([got, keep], axis=0), jnp.concatenate([keep, got], axis=0)
    )


def exclusive_scan(state, logs, axis, forward):
    count = lax.axis_size(axis)
    levels = []
    for bit in (1, 2):
        state, logs, saved = pair_down(state, logs, axis, bit, forward)
        levels.append((bit, saved))
    stride = 4
    groups = count // stride
    window_state, window_log = send_with_logs(state, logs, axis, shift_perm(count, stride, forward))
    width = 1
    while width < groups:
        perm = shift_perm(count, stride * width, forward)
        if width * 2 < groups:
            got_state, got_log = send_with_logs(window_state, window_log, axis, perm)
            window_log_next = window_log + got_log
        else:
            got_state = lax.ppermute(window_state, axis, perm)
            window_log_next = window_log
        window_state = window_state + jnp.exp(window_log)[:, None, None] * got_state
        window_log = window_log_next
        width *= 2
    for bit, saved in reversed(levels):
        window_state = pair_up(window_state, saved, axis, bit, forward)
    return window_state


def split_bf16(value):
    upper = lax.reduce_precision(value, exponent_bits=8, mantissa_bits=7)
    return upper.astype(jnp.bfloat16), (value - upper).astype(jnp.bfloat16)


def mp_sum_scatter(value, axis):
    count = lax.axis_size(axis)
    blocks = value.reshape(count, value.shape[0] // count, value.shape[1])
    return jnp.sum(lax.all_to_all(blocks, axis, 0, 0), axis=0)


def attend_kernel(first_ref, query_ref, key_ref, upper_ref, lower_ref, out_ref, top_ref, total_ref, mix_ref, *, heads):
    block = pl.program_id(0)
    rows = query_ref.shape[0]
    width = query_ref.shape[1]
    keys_per_block = key_ref.shape[0]
    first = first_ref[0]

    @pl.when(block == 0)
    def _():
        top_ref[...] = jnp.full(top_ref.shape, very_negative, jnp.float32)
        total_ref[...] = jnp.zeros(total_ref.shape, jnp.float32)
        mix_ref[...] = jnp.zeros(mix_ref.shape, jnp.float32)

    @pl.when(block * keys_per_block <= first + rows // heads - 1)
    def _():
        scores = lax.dot_general(
            query_ref[...], key_ref[...], (((1,), (1,)), ((), ())), preferred_element_type=jnp.float32
        ) / math.sqrt(width)
        row = lax.broadcasted_iota(jnp.int32, scores.shape, 0)
        col = lax.broadcasted_iota(jnp.int32, scores.shape, 1)
        allowed = block * keys_per_block + col <= first + row // heads
        scores = jnp.where(allowed, scores, very_negative)
        top_old = top_ref[...]
        top_new = jnp.maximum(top_old, jnp.max(scores, axis=1, keepdims=True))
        rescale = jnp.exp(top_old - top_new)
        weights = jnp.where(allowed, jnp.exp(scores - top_new), 0.0)
        total_ref[...] = rescale * total_ref[...] + jnp.sum(weights, axis=1, keepdims=True)
        weights_hi = weights.astype(jnp.bfloat16)
        weights_lo = (weights - weights_hi.astype(jnp.float32)).astype(jnp.bfloat16)
        upper = upper_ref[...]
        mixed = (
            jnp.dot(weights_hi, upper, preferred_element_type=jnp.float32)
            + jnp.dot(weights_hi, lower_ref[...], preferred_element_type=jnp.float32)
            + jnp.dot(weights_lo, upper, preferred_element_type=jnp.float32)
        )
        mix_ref[...] = rescale * mix_ref[...] + mixed
        top_ref[...] = top_new

    @pl.when(block == pl.num_programs(0) - 1)
    def _():
        out_ref[...] = mix_ref[...] / total_ref[...]


def attend(first_query, query_rows, every, heads, keys_per_block=512):
    rows, width = query_rows.shape
    blocks = every.shape[0] // keys_per_block
    flops = 2 * rows * every.shape[0] * width * 4
    return pl.pallas_call(
        functools.partial(attend_kernel, heads=heads),
        out_shape=jax.ShapeDtypeStruct((rows, width), jnp.float32),
        grid_spec=pltpu.PrefetchScalarGridSpec(
            num_scalar_prefetch=1,
            grid=(blocks,),
            in_specs=[
                pl.BlockSpec((rows, width), lambda b, f: (0, 0)),
                pl.BlockSpec((keys_per_block, width), lambda b, f: (b, 0)),
                pl.BlockSpec((keys_per_block, width), lambda b, f: (b, 1)),
                pl.BlockSpec((keys_per_block, width), lambda b, f: (b, 2)),
            ],
            out_specs=pl.BlockSpec((rows, width), lambda b, f: (0, 0)),
            scratch_shapes=[
                pltpu.VMEM((rows, 1), jnp.float32),
                pltpu.VMEM((rows, 1), jnp.float32),
                pltpu.VMEM((rows, width), jnp.float32),
            ],
        ),
        compiler_params=pltpu.CompilerParams(dimension_semantics=("arbitrary",)),
        cost_estimate=pl.CostEstimate(
            flops=flops,
            transcendentals=rows * every.shape[0],
            bytes_accessed=every.size * 2 + query_rows.size * 2 + rows * width * 4,
        ),
    )(first_query, query_rows, every, every, every)


def local(queries, keys, values, inputs_x, in_b, in_c, log_decay):
    row_count = queries.shape[0]
    heads = queries.shape[1] // HEAD_WIDTH
    seq_count = lax.axis_size("seq")
    own_index = lax.axis_index("seq")
    first_query = own_index * row_count

    values_hi, values_lo = split_bf16(values)
    packed = jnp.concatenate([keys, values_hi, values_lo], axis=1)
    every = lax.all_gather(packed, "seq", axis=0, tiled=True)

    c_scale = 0.5 / math.sqrt(N * row_count * seq_count)
    student_x = inputs_x.astype(jnp.float32).reshape(row_count, heads, HEAD_WIDTH)
    b_rows = in_b.astype(jnp.float32)
    c_rows = in_c.astype(jnp.float32) * c_scale
    cumulative = jnp.cumsum(log_decay, axis=0)
    totals = cumulative[-1]
    heads_first = cumulative.T
    causal = jnp.arange(row_count)[:, None] >= jnp.arange(row_count)[None, :]
    decays = jnp.exp(
        jnp.where(causal[None], heads_first[:, :, None] - heads_first[:, None, :], -jnp.inf)
    )
    inner_products = jnp.dot(in_c, in_b.T, preferred_element_type=jnp.float32) * c_scale
    mixing = decays * inner_products[None]
    rising = jnp.exp(cumulative)
    ending = jnp.exp(totals[None, :] - cumulative)
    local_state = jnp.einsum(
        "shp,sn->hpn", student_x * ending[:, :, None], b_rows, precision=highest
    )
    state_in = exclusive_scan(local_state, totals, "seq", True)

    query_rows = queries.reshape(row_count * heads, HEAD_WIDTH)
    teacher_out = attend(
        jnp.reshape(first_query, (1,)).astype(jnp.int32), query_rows, every, heads
    ).reshape(row_count, heads, HEAD_WIDTH)

    y_intra = jnp.einsum("hts,shp->thp", mixing, student_x, precision=highest)
    y_inter = jnp.einsum("tn,hpn->thp", c_rows, state_in, precision=highest) * rising[:, :, None]
    mismatch = y_intra + y_inter - teacher_out
    scaled_mismatch = mismatch * rising[:, :, None]
    local_grad = jnp.einsum("thp,tn->hpn", scaled_mismatch, c_rows, precision=highest)
    later_grad = exclusive_scan(local_grad, totals, "seq", False)
    grad_x = jnp.einsum("hts,thp->shp", mixing, mismatch, precision=highest)
    grad_x = (
        grad_x
        + jnp.einsum("hpn,sn->shp", later_grad, b_rows, precision=highest) * ending[:, :, None]
    )
    products = jnp.einsum("thp,shp->hts", mismatch, student_x, precision=highest)
    weighted = decays * products
    grad_b = jnp.einsum("hts,tn->sn", weighted, c_rows, precision=highest)
    grad_b = grad_b + jnp.einsum(
        "shp,hpn->sn", student_x * ending[:, :, None], later_grad, precision=highest
    )
    grad_c = jnp.einsum("hts,sn->tn", weighted, b_rows, precision=highest)
    grad_c = grad_c + jnp.einsum("thp,hpn->tn", scaled_mismatch, state_in, precision=highest)
    summed = mp_sum_scatter(jnp.concatenate([grad_b, grad_c], axis=1), "mp")
    summed_b, summed_c = summed[:, :N], summed[:, N:]
    return (grad_x.reshape(row_count, heads * HEAD_WIDTH), summed_b, summed_c * c_scale)


def solution(mesh):
    in_specs = (
        P("seq", "mp"),
        P("seq", "mp"),
        P("seq", "mp"),
        P("seq", "mp"),
        P("seq", None),
        P("seq", None),
        P("seq", "mp"),
    )
    out_specs = (P("seq", "mp"), P(("seq", "mp"), None), P(("seq", "mp"), None))
    return jax.shard_map(local, mesh=mesh, in_specs=in_specs, out_specs=out_specs, check_vma=False)
```

```python
import functools
import math

import jax
import jax.numpy as jnp
from jax import lax
from jax.experimental import pallas as pl
from jax.experimental.pallas import tpu as pltpu
from jax.sharding import PartitionSpec as P

HEAD_WIDTH = 128
N = 128

very_negative = -1e30
highest = lax.Precision.HIGHEST


def shift(value, axis, distance, forward):
    count = lax.axis_size(axis)
    if forward:
        perm = [(j, j + distance) for j in range(count - distance)]
    else:
        perm = [(j + distance, j) for j in range(count - distance)]
    return lax.ppermute(value, axis, perm)


def send_with_logs(state, logs, axis, perm):
    heads, rows, width = state.shape
    count = logs.shape[0]
    log_rows = jnp.pad(jnp.broadcast_to(logs[:, None], (count, width)), ((0, -count % 8), (0, 0)))
    payload = jnp.concatenate([state.reshape(heads * rows, width), log_rows], axis=0)
    got = lax.ppermute(payload, axis, perm)
    return got[: heads * rows].reshape(heads, rows, width), got[heads * rows : heads * rows + count, 0]


def shift_perm(count, distance, forward):
    if forward:
        return [(j, j + distance) for j in range(count - distance)]
    return [(j + distance, j) for j in range(count - distance)]


def pair_down(state, logs, axis, bit, forward):
    count = lax.axis_size(axis)
    upper = (lax.axis_index(axis) // bit) % 2 == 1
    first = jnp.logical_not(upper) if forward else upper
    half = state.shape[0] // 2
    mine = jnp.where(upper, half, 0)
    other = half - mine
    own_state = lax.dynamic_slice_in_dim(state, mine, half, axis=0)
    own_logs = lax.dynamic_slice_in_dim(logs, mine, half)
    got_state, got_logs = send_with_logs(
        lax.dynamic_slice_in_dim(state, other, half, axis=0),
        lax.dynamic_slice_in_dim(logs, other, half),
        axis,
        [(j, j ^ bit) for j in range(count)],
    )
    first_state = jnp.where(first, own_state, got_state)
    second_state = jnp.where(first, got_state, own_state)
    first_logs = jnp.where(first, own_logs, got_logs)
    second_logs = jnp.where(first, got_logs, own_logs)
    pair_state = jnp.exp(second_logs)[:, None, None] * first_state + second_state
    return pair_state, first_logs + second_logs, (first_state, first_logs)


def pair_up(window, saved, axis, bit, forward):
    count = lax.axis_size(axis)
    upper = (lax.axis_index(axis) // bit) % 2 == 1
    first = jnp.logical_not(upper) if forward else upper
    first_state, first_logs = saved
    second_window = jnp.exp(first_logs)[:, None, None] * window + first_state
    keep = jnp.where(first, window, second_window)
    send = jnp.where(first, second_window, window)
    got = lax.ppermute(send, axis, [(j, j ^ bit) for j in range(count)])
    return jnp.where(
        upper, jnp.concatenate([got, keep], axis=0), jnp.concatenate([keep, got], axis=0)
    )


def exclusive_scan(state, logs, axis, forward):
    count = lax.axis_size(axis)
    levels = []
    for bit in (1, 2):
        state, logs, saved = pair_down(state, logs, axis, bit, forward)
        levels.append((bit, saved))
    stride = 4
    groups = count // stride
    window_state, window_log = send_with_logs(state, logs, axis, shift_perm(count, stride, forward))
    width = 1
    while width < groups:
        perm = shift_perm(count, stride * width, forward)
        if width * 2 < groups:
            got_state, got_log = send_with_logs(window_state, window_log, axis, perm)
            window_log_next = window_log + got_log
        else:
            got_state = lax.ppermute(window_state, axis, perm)
            window_log_next = window_log
        window_state = window_state + jnp.exp(window_log)[:, None, None] * got_state
        window_log = window_log_next
        width *= 2
    for bit, saved in reversed(levels):
        window_state = pair_up(window_state, saved, axis, bit, forward)
    return window_state


def gather_blocks(block, axis):
    count = lax.axis_size(axis)
    index = lax.axis_index(axis)
    pieces = block
    for bit in (1, 2):
        got = lax.ppermute(pieces, axis, [(j, j ^ bit) for j in range(count)])
        upper = (index // bit) % 2 == 1
        pieces = jnp.where(
            upper, jnp.concatenate([got, pieces], axis=0), jnp.concatenate([pieces, got], axis=0)
        )
    groups = [[z * 4 + r for z in range(count // 4)] for r in range(4)]
    return lax.all_gather(pieces, axis, axis=0, tiled=True, axis_index_groups=groups)


def split_bf16(value):
    upper = lax.reduce_precision(value, exponent_bits=8, mantissa_bits=7)
    return upper.astype(jnp.bfloat16), (value - upper).astype(jnp.bfloat16)


def mp_sum_scatter(value, axis):
    count = lax.axis_size(axis)
    blocks = value.reshape(count, value.shape[0] // count, value.shape[1])
    return jnp.sum(lax.all_to_all(blocks, axis, 0, 0), axis=0)


def attend_kernel(first_ref, query_ref, key_ref, upper_ref, lower_ref, out_ref, top_ref, total_ref, mix_ref, *, heads):
    block = pl.program_id(0)
    rows = query_ref.shape[0]
    width = query_ref.shape[1]
    keys_per_block = key_ref.shape[0]
    first = first_ref[0]

    @pl.when(block == 0)
    def _():
        top_ref[...] = jnp.full(top_ref.shape, very_negative, jnp.float32)
        total_ref[...] = jnp.zeros(total_ref.shape, jnp.float32)
        mix_ref[...] = jnp.zeros(mix_ref.shape, jnp.float32)

    @pl.when(block * keys_per_block <= first + rows // heads - 1)
    def _():
        scores = lax.dot_general(
            query_ref[...], key_ref[...], (((1,), (1,)), ((), ())), preferred_element_type=jnp.float32
        ) / math.sqrt(width)
        row = lax.broadcasted_iota(jnp.int32, scores.shape, 0)
        col = lax.broadcasted_iota(jnp.int32, scores.shape, 1)
        allowed = block * keys_per_block + col <= first + row // heads
        scores = jnp.where(allowed, scores, very_negative)
        top_old = top_ref[...]
        top_new = jnp.maximum(top_old, jnp.max(scores, axis=1, keepdims=True))
        rescale = jnp.exp(top_old - top_new)
        weights = jnp.where(allowed, jnp.exp(scores - top_new), 0.0)
        total_ref[...] = rescale * total_ref[...] + jnp.sum(weights, axis=1, keepdims=True)
        weights_hi = weights.astype(jnp.bfloat16)
        weights_lo = (weights - weights_hi.astype(jnp.float32)).astype(jnp.bfloat16)
        upper = upper_ref[...]
        mixed = (
            jnp.dot(weights_hi, upper, preferred_element_type=jnp.float32)
            + jnp.dot(weights_hi, lower_ref[...], preferred_element_type=jnp.float32)
            + jnp.dot(weights_lo, upper, preferred_element_type=jnp.float32)
        )
        mix_ref[...] = rescale * mix_ref[...] + mixed
        top_ref[...] = top_new

    @pl.when(block == pl.num_programs(0) - 1)
    def _():
        out_ref[...] = mix_ref[...] / total_ref[...]


def attend(first_query, query_rows, every, heads, keys_per_block=512):
    rows, width = query_rows.shape
    blocks = every.shape[0] // keys_per_block
    flops = 2 * rows * every.shape[0] * width * 4
    return pl.pallas_call(
        functools.partial(attend_kernel, heads=heads),
        out_shape=jax.ShapeDtypeStruct((rows, width), jnp.float32),
        grid_spec=pltpu.PrefetchScalarGridSpec(
            num_scalar_prefetch=1,
            grid=(blocks,),
            in_specs=[
                pl.BlockSpec((rows, width), lambda b, f: (0, 0)),
                pl.BlockSpec((keys_per_block, width), lambda b, f: (b, 0)),
                pl.BlockSpec((keys_per_block, width), lambda b, f: (b, 1)),
                pl.BlockSpec((keys_per_block, width), lambda b, f: (b, 2)),
            ],
            out_specs=pl.BlockSpec((rows, width), lambda b, f: (0, 0)),
            scratch_shapes=[
                pltpu.VMEM((rows, 1), jnp.float32),
                pltpu.VMEM((rows, 1), jnp.float32),
                pltpu.VMEM((rows, width), jnp.float32),
            ],
        ),
        compiler_params=pltpu.CompilerParams(dimension_semantics=("arbitrary",)),
        cost_estimate=pl.CostEstimate(
            flops=flops,
            transcendentals=rows * every.shape[0],
            bytes_accessed=every.size * 2 + query_rows.size * 2 + rows * width * 4,
        ),
    )(first_query, query_rows, every, every, every)


def local(queries, keys, values, inputs_x, in_b, in_c, log_decay):
    row_count = queries.shape[0]
    heads = queries.shape[1] // HEAD_WIDTH
    seq_count = lax.axis_size("seq")
    own_index = lax.axis_index("seq")
    first_query = own_index * row_count

    values_hi, values_lo = split_bf16(values)
    packed = jnp.concatenate([keys, values_hi, values_lo], axis=1)
    every = gather_blocks(packed, "seq")

    c_scale = 0.5 / math.sqrt(N * row_count * seq_count)
    student_x = inputs_x.astype(jnp.float32).reshape(row_count, heads, HEAD_WIDTH)
    b_rows = in_b.astype(jnp.float32)
    c_rows = in_c.astype(jnp.float32) * c_scale
    cumulative = jnp.cumsum(log_decay, axis=0)
    totals = cumulative[-1]
    heads_first = cumulative.T
    causal = jnp.arange(row_count)[:, None] >= jnp.arange(row_count)[None, :]
    decays = jnp.exp(
        jnp.where(causal[None], heads_first[:, :, None] - heads_first[:, None, :], -jnp.inf)
    )
    inner_products = jnp.dot(in_c, in_b.T, preferred_element_type=jnp.float32) * c_scale
    mixing = decays * inner_products[None]
    rising = jnp.exp(cumulative)
    ending = jnp.exp(totals[None, :] - cumulative)
    local_state = jnp.einsum(
        "shp,sn->hpn", student_x * ending[:, :, None], b_rows, precision=highest
    )
    state_in = exclusive_scan(local_state, totals, "seq", True)

    query_rows = queries.reshape(row_count * heads, HEAD_WIDTH)
    teacher_out = attend(
        jnp.reshape(first_query, (1,)).astype(jnp.int32), query_rows, every, heads
    ).reshape(row_count, heads, HEAD_WIDTH)

    y_intra = jnp.einsum("hts,shp->thp", mixing, student_x, precision=highest)
    y_inter = jnp.einsum("tn,hpn->thp", c_rows, state_in, precision=highest) * rising[:, :, None]
    mismatch = y_intra + y_inter - teacher_out
    scaled_mismatch = mismatch * rising[:, :, None]
    local_grad = jnp.einsum("thp,tn->hpn", scaled_mismatch, c_rows, precision=highest)
    later_grad = exclusive_scan(local_grad, totals, "seq", False)
    grad_x = jnp.einsum("hts,thp->shp", mixing, mismatch, precision=highest)
    grad_x = (
        grad_x
        + jnp.einsum("hpn,sn->shp", later_grad, b_rows, precision=highest) * ending[:, :, None]
    )
    products = jnp.einsum("thp,shp->hts", mismatch, student_x, precision=highest)
    weighted = decays * products
    grad_b = jnp.einsum("hts,tn->sn", weighted, c_rows, precision=highest)
    grad_b = grad_b + jnp.einsum(
        "shp,hpn->sn", student_x * ending[:, :, None], later_grad, precision=highest
    )
    grad_c = jnp.einsum("hts,sn->tn", weighted, b_rows, precision=highest)
    grad_c = grad_c + jnp.einsum("thp,hpn->tn", scaled_mismatch, state_in, precision=highest)
    summed = mp_sum_scatter(jnp.concatenate([grad_b, grad_c], axis=1), "mp")
    summed_b, summed_c = summed[:, :N], summed[:, N:]
    return (grad_x.reshape(row_count, heads * HEAD_WIDTH), summed_b, summed_c * c_scale)


def solution(mesh):
    in_specs = (
        P("seq", "mp"),
        P("seq", "mp"),
        P("seq", "mp"),
        P("seq", "mp"),
        P("seq", None),
        P("seq", None),
        P("seq", "mp"),
    )
    out_specs = (P("seq", "mp"), P(("seq", "mp"), None), P(("seq", "mp"), None))
    return jax.shard_map(local, mesh=mesh, in_specs=in_specs, out_specs=out_specs, check_vma=False)
```

```python
import functools
import math

import jax
import jax.numpy as jnp
from jax import lax
from jax.experimental import pallas as pl
from jax.experimental.pallas import tpu as pltpu
from jax.sharding import PartitionSpec as P

HEAD_WIDTH = 128
N = 128

very_negative = -1e30
highest = lax.Precision.HIGHEST


def shift(value, axis, distance, forward):
    count = lax.axis_size(axis)
    if forward:
        perm = [(j, j + distance) for j in range(count - distance)]
    else:
        perm = [(j + distance, j) for j in range(count - distance)]
    return lax.ppermute(value, axis, perm)


def send_with_logs(state, logs, axis, perm):
    heads, rows, width = state.shape
    count = logs.shape[0]
    log_rows = jnp.pad(jnp.broadcast_to(logs[:, None], (count, width)), ((0, -count % 8), (0, 0)))
    payload = jnp.concatenate([state.reshape(heads * rows, width), log_rows], axis=0)
    got = lax.ppermute(payload, axis, perm)
    return got[: heads * rows].reshape(heads, rows, width), got[heads * rows : heads * rows + count, 0]


def shift_perm(count, distance, forward):
    if forward:
        return [(j, j + distance) for j in range(count - distance)]
    return [(j + distance, j) for j in range(count - distance)]


def pair_down(state, logs, axis, bit, forward):
    count = lax.axis_size(axis)
    upper = (lax.axis_index(axis) // bit) % 2 == 1
    first = jnp.logical_not(upper) if forward else upper
    half = state.shape[0] // 2
    mine = jnp.where(upper, half, 0)
    other = half - mine
    own_state = lax.dynamic_slice_in_dim(state, mine, half, axis=0)
    own_logs = lax.dynamic_slice_in_dim(logs, mine, half)
    got_state, got_logs = send_with_logs(
        lax.dynamic_slice_in_dim(state, other, half, axis=0),
        lax.dynamic_slice_in_dim(logs, other, half),
        axis,
        [(j, j ^ bit) for j in range(count)],
    )
    first_state = jnp.where(first, own_state, got_state)
    second_state = jnp.where(first, got_state, own_state)
    first_logs = jnp.where(first, own_logs, got_logs)
    second_logs = jnp.where(first, got_logs, own_logs)
    pair_state = jnp.exp(second_logs)[:, None, None] * first_state + second_state
    return pair_state, first_logs + second_logs, (first_state, first_logs)


def pair_up(window, saved, axis, bit, forward):
    count = lax.axis_size(axis)
    upper = (lax.axis_index(axis) // bit) % 2 == 1
    first = jnp.logical_not(upper) if forward else upper
    first_state, first_logs = saved
    second_window = jnp.exp(first_logs)[:, None, None] * window + first_state
    keep = jnp.where(first, window, second_window)
    send = jnp.where(first, second_window, window)
    got = lax.ppermute(send, axis, [(j, j ^ bit) for j in range(count)])
    return jnp.where(
        upper, jnp.concatenate([got, keep], axis=0), jnp.concatenate([keep, got], axis=0)
    )


def exclusive_scan(state, logs, axis, forward):
    count = lax.axis_size(axis)
    levels = []
    for bit in (1, 2):
        state, logs, saved = pair_down(state, logs, axis, bit, forward)
        levels.append((bit, saved))
    stride = 4
    groups = count // stride
    window_state, window_log = send_with_logs(state, logs, axis, shift_perm(count, stride, forward))
    width = 1
    while width < groups:
        perm = shift_perm(count, stride * width, forward)
        if width * 2 < groups:
            got_state, got_log = send_with_logs(window_state, window_log, axis, perm)
            window_log_next = window_log + got_log
        else:
            got_state = lax.ppermute(window_state, axis, perm)
            window_log_next = window_log
        window_state = window_state + jnp.exp(window_log)[:, None, None] * got_state
        window_log = window_log_next
        width *= 2
    for bit, saved in reversed(levels):
        window_state = pair_up(window_state, saved, axis, bit, forward)
    return window_state


def gather_blocks(block, axis):
    count = lax.axis_size(axis)
    index = lax.axis_index(axis)
    pieces = block
    for bit in (1, 2):
        got = lax.ppermute(pieces, axis, [(j, j ^ bit) for j in range(count)])
        upper = (index // bit) % 2 == 1
        pieces = jnp.where(
            upper, jnp.concatenate([got, pieces], axis=0), jnp.concatenate([pieces, got], axis=0)
        )
    groups = [[z * 4 + r for z in range(count // 4)] for r in range(4)]
    return lax.all_gather(pieces, axis, axis=0, tiled=True, axis_index_groups=groups)


def split_bf16(value):
    upper = lax.reduce_precision(value, exponent_bits=8, mantissa_bits=7)
    return upper.astype(jnp.bfloat16), (value - upper).astype(jnp.bfloat16)


def mp_sum_scatter(value, axis):
    count = lax.axis_size(axis)
    blocks = value.reshape(count, value.shape[0] // count, value.shape[1])
    return jnp.sum(lax.all_to_all(blocks, axis, 0, 0), axis=0)


def attend_kernel(first_ref, query_ref, key_ref, upper_ref, lower_ref, out_ref, top_ref, total_ref, mix_ref, *, heads):
    block = pl.program_id(0)
    rows = query_ref.shape[0]
    width = query_ref.shape[1]
    keys_per_block = key_ref.shape[0]
    first = first_ref[0]

    @pl.when(block == 0)
    def _():
        top_ref[...] = jnp.full(top_ref.shape, very_negative, jnp.float32)
        total_ref[...] = jnp.zeros(total_ref.shape, jnp.float32)
        mix_ref[...] = jnp.zeros(mix_ref.shape, jnp.float32)

    def accumulate(masked):
        scores = lax.dot_general(
            query_ref[...], key_ref[...], (((1,), (1,)), ((), ())), preferred_element_type=jnp.float32
        ) * (1.0 / math.sqrt(width))
        if masked:
            row = lax.broadcasted_iota(jnp.int32, scores.shape, 0)
            col = lax.broadcasted_iota(jnp.int32, scores.shape, 1)
            allowed = block * keys_per_block + col <= first + row // heads
            scores = jnp.where(allowed, scores, very_negative)
        top_old = top_ref[...]
        top_new = jnp.maximum(top_old, jnp.max(scores, axis=1, keepdims=True))
        rescale = jnp.exp(top_old - top_new)
        weights = jnp.exp(scores - top_new)
        if masked:
            weights = jnp.where(allowed, weights, 0.0)
        total_ref[...] = rescale * total_ref[...] + jnp.sum(weights, axis=1, keepdims=True)
        weights_hi = weights.astype(jnp.bfloat16)
        weights_lo = (weights - weights_hi.astype(jnp.float32)).astype(jnp.bfloat16)
        upper = upper_ref[...]
        mixed = (
            jnp.dot(weights_hi, upper, preferred_element_type=jnp.float32)
            + jnp.dot(weights_hi, lower_ref[...], preferred_element_type=jnp.float32)
            + jnp.dot(weights_lo, upper, preferred_element_type=jnp.float32)
        )
        mix_ref[...] = rescale * mix_ref[...] + mixed
        top_ref[...] = top_new

    block_end = (block + 1) * keys_per_block - 1

    @pl.when(block_end <= first)
    def _():
        accumulate(False)

    @pl.when(jnp.logical_and(block_end > first, block * keys_per_block <= first + rows // heads - 1))
    def _():
        accumulate(True)

    @pl.when(block == pl.num_programs(0) - 1)
    def _():
        out_ref[...] = mix_ref[...] / total_ref[...]


def attend(first_query, query_rows, every, heads, keys_per_block=512):
    rows, width = query_rows.shape
    blocks = every.shape[0] // keys_per_block
    flops = 2 * rows * every.shape[0] * width * 4
    return pl.pallas_call(
        functools.partial(attend_kernel, heads=heads),
        out_shape=jax.ShapeDtypeStruct((rows, width), jnp.float32),
        grid_spec=pltpu.PrefetchScalarGridSpec(
            num_scalar_prefetch=1,
            grid=(blocks,),
            in_specs=[
                pl.BlockSpec((rows, width), lambda b, f: (0, 0)),
                pl.BlockSpec((keys_per_block, width), lambda b, f: (b, 0)),
                pl.BlockSpec((keys_per_block, width), lambda b, f: (b, 1)),
                pl.BlockSpec((keys_per_block, width), lambda b, f: (b, 2)),
            ],
            out_specs=pl.BlockSpec((rows, width), lambda b, f: (0, 0)),
            scratch_shapes=[
                pltpu.VMEM((rows, 1), jnp.float32),
                pltpu.VMEM((rows, 1), jnp.float32),
                pltpu.VMEM((rows, width), jnp.float32),
            ],
        ),
        compiler_params=pltpu.CompilerParams(dimension_semantics=("arbitrary",)),
        cost_estimate=pl.CostEstimate(
            flops=flops,
            transcendentals=rows * every.shape[0],
            bytes_accessed=every.size * 2 + query_rows.size * 2 + rows * width * 4,
        ),
    )(first_query, query_rows, every, every, every)


def local(queries, keys, values, inputs_x, in_b, in_c, log_decay):
    row_count = queries.shape[0]
    heads = queries.shape[1] // HEAD_WIDTH
    seq_count = lax.axis_size("seq")
    own_index = lax.axis_index("seq")
    first_query = own_index * row_count

    values_hi, values_lo = split_bf16(values)
    packed = jnp.concatenate([keys, values_hi, values_lo], axis=1)
    every = gather_blocks(packed, "seq")

    c_scale = 0.5 / math.sqrt(N * row_count * seq_count)
    student_x = inputs_x.astype(jnp.float32).reshape(row_count, heads, HEAD_WIDTH)
    b_rows = in_b.astype(jnp.float32)
    c_rows = in_c.astype(jnp.float32) * c_scale
    cumulative = jnp.cumsum(log_decay, axis=0)
    totals = cumulative[-1]
    heads_first = cumulative.T
    causal = jnp.arange(row_count)[:, None] >= jnp.arange(row_count)[None, :]
    decays = jnp.exp(
        jnp.where(causal[None], heads_first[:, :, None] - heads_first[:, None, :], -jnp.inf)
    )
    inner_products = jnp.dot(in_c, in_b.T, preferred_element_type=jnp.float32) * c_scale
    mixing = decays * inner_products[None]
    rising = jnp.exp(cumulative)
    ending = jnp.exp(totals[None, :] - cumulative)
    local_state = jnp.einsum(
        "shp,sn->hpn", student_x * ending[:, :, None], b_rows, precision=highest
    )
    state_in = exclusive_scan(local_state, totals, "seq", True)

    query_rows = queries.reshape(row_count * heads, HEAD_WIDTH)
    teacher_out = attend(
        jnp.reshape(first_query, (1,)).astype(jnp.int32), query_rows, every, heads
    ).reshape(row_count, heads, HEAD_WIDTH)

    y_intra = jnp.einsum("hts,shp->thp", mixing, student_x, precision=highest)
    y_inter = jnp.einsum("tn,hpn->thp", c_rows, state_in, precision=highest) * rising[:, :, None]
    mismatch = y_intra + y_inter - teacher_out
    scaled_mismatch = mismatch * rising[:, :, None]
    local_grad = jnp.einsum("thp,tn->hpn", scaled_mismatch, c_rows, precision=highest)
    later_grad = exclusive_scan(local_grad, totals, "seq", False)
    grad_x = jnp.einsum("hts,thp->shp", mixing, mismatch, precision=highest)
    grad_x = (
        grad_x
        + jnp.einsum("hpn,sn->shp", later_grad, b_rows, precision=highest) * ending[:, :, None]
    )
    products = jnp.einsum("thp,shp->hts", mismatch, student_x, precision=highest)
    weighted = decays * products
    grad_b = jnp.einsum("hts,tn->sn", weighted, c_rows, precision=highest)
    grad_b = grad_b + jnp.einsum(
        "shp,hpn->sn", student_x * ending[:, :, None], later_grad, precision=highest
    )
    grad_c = jnp.einsum("hts,sn->tn", weighted, b_rows, precision=highest)
    grad_c = grad_c + jnp.einsum("thp,hpn->tn", scaled_mismatch, state_in, precision=highest)
    summed = mp_sum_scatter(jnp.concatenate([grad_b, grad_c], axis=1), "mp")
    summed_b, summed_c = summed[:, :N], summed[:, N:]
    return (grad_x.reshape(row_count, heads * HEAD_WIDTH), summed_b, summed_c * c_scale)


def solution(mesh):
    in_specs = (
        P("seq", "mp"),
        P("seq", "mp"),
        P("seq", "mp"),
        P("seq", "mp"),
        P("seq", None),
        P("seq", None),
        P("seq", "mp"),
    )
    out_specs = (P("seq", "mp"), P(("seq", "mp"), None), P(("seq", "mp"), None))
    return jax.shard_map(local, mesh=mesh, in_specs=in_specs, out_specs=out_specs, check_vma=False)
```

```python
import functools
import math

import jax
import jax.numpy as jnp
from jax import lax
from jax.experimental import pallas as pl
from jax.experimental.pallas import tpu as pltpu
from jax.sharding import PartitionSpec as P

HEAD_WIDTH = 128
N = 128

very_negative = -1e30
highest = lax.Precision.HIGHEST


def shift(value, axis, distance, forward):
    count = lax.axis_size(axis)
    if forward:
        perm = [(j, j + distance) for j in range(count - distance)]
    else:
        perm = [(j + distance, j) for j in range(count - distance)]
    return lax.ppermute(value, axis, perm)


def send_with_logs(state, logs, axis, perm, extra=None):
    heads, rows, width = state.shape
    count = logs.shape[0]
    log_rows = jnp.pad(jnp.broadcast_to(logs[:, None], (count, width)), ((0, -count % 8), (0, 0)))
    payload = jnp.concatenate([state.reshape(heads * rows, width), log_rows], axis=0)
    if extra is None:
        got = lax.ppermute(payload, axis, perm)
        got_extra = None
    else:
        got, got_extra = lax.ppermute((payload, extra), axis, perm)
    got_state = got[: heads * rows].reshape(heads, rows, width)
    got_logs = got[heads * rows : heads * rows + count, 0]
    if extra is None:
        return got_state, got_logs
    return got_state, got_logs, got_extra


def shift_perm(count, distance, forward):
    if forward:
        return [(j, j + distance) for j in range(count - distance)]
    return [(j + distance, j) for j in range(count - distance)]


def pair_down(state, logs, axis, bit, forward, extra=None):
    count = lax.axis_size(axis)
    upper = (lax.axis_index(axis) // bit) % 2 == 1
    first = jnp.logical_not(upper) if forward else upper
    half = state.shape[0] // 2
    mine = jnp.where(upper, half, 0)
    other = half - mine
    own_state = lax.dynamic_slice_in_dim(state, mine, half, axis=0)
    own_logs = lax.dynamic_slice_in_dim(logs, mine, half)
    sent = send_with_logs(
        lax.dynamic_slice_in_dim(state, other, half, axis=0),
        lax.dynamic_slice_in_dim(logs, other, half),
        axis,
        [(j, j ^ bit) for j in range(count)],
        extra,
    )
    got_state, got_logs = sent[:2]
    joined = None
    if extra is not None:
        joined = sent[2]
        joined = jnp.where(
            upper, jnp.concatenate([joined, extra], axis=0), jnp.concatenate([extra, joined], axis=0)
        )
    first_state = jnp.where(first, own_state, got_state)
    second_state = jnp.where(first, got_state, own_state)
    first_logs = jnp.where(first, own_logs, got_logs)
    second_logs = jnp.where(first, got_logs, own_logs)
    pair_state = jnp.exp(second_logs)[:, None, None] * first_state + second_state
    return pair_state, first_logs + second_logs, (first_state, first_logs), joined


def pair_up(window, saved, axis, bit, forward):
    count = lax.axis_size(axis)
    upper = (lax.axis_index(axis) // bit) % 2 == 1
    first = jnp.logical_not(upper) if forward else upper
    first_state, first_logs = saved
    second_window = jnp.exp(first_logs)[:, None, None] * window + first_state
    keep = jnp.where(first, window, second_window)
    send = jnp.where(first, second_window, window)
    got = lax.ppermute(send, axis, [(j, j ^ bit) for j in range(count)])
    return jnp.where(
        upper, jnp.concatenate([got, keep], axis=0), jnp.concatenate([keep, got], axis=0)
    )


def exclusive_scan(state, logs, axis, forward, extra=None):
    count = lax.axis_size(axis)
    levels = []
    for bit in (1, 2):
        state, logs, saved, extra = pair_down(state, logs, axis, bit, forward, extra)
        levels.append((bit, saved))
    stride = 4
    groups = count // stride
    window_state, window_log = send_with_logs(state, logs, axis, shift_perm(count, stride, forward))
    width = 1
    while width < groups:
        perm = shift_perm(count, stride * width, forward)
        if width * 2 < groups:
            got_state, got_log = send_with_logs(window_state, window_log, axis, perm)
            window_log_next = window_log + got_log
        else:
            got_state = lax.ppermute(window_state, axis, perm)
            window_log_next = window_log
        window_state = window_state + jnp.exp(window_log)[:, None, None] * got_state
        window_log = window_log_next
        width *= 2
    for bit, saved in reversed(levels):
        window_state = pair_up(window_state, saved, axis, bit, forward)
    return window_state, extra


def gather_groups(pieces, axis):
    count = lax.axis_size(axis)
    groups = [[z * 4 + r for z in range(count // 4)] for r in range(4)]
    return lax.all_gather(pieces, axis, axis=0, tiled=True, axis_index_groups=groups)


def split_bf16(value):
    upper = lax.reduce_precision(value, exponent_bits=8, mantissa_bits=7)
    return upper.astype(jnp.bfloat16), (value - upper).astype(jnp.bfloat16)


def mp_sum_scatter(value, axis):
    count = lax.axis_size(axis)
    blocks = value.reshape(count, value.shape[0] // count, value.shape[1])
    return jnp.sum(lax.all_to_all(blocks, axis, 0, 0), axis=0)


def attend_kernel(first_ref, query_ref, key_ref, upper_ref, lower_ref, out_ref, top_ref, total_ref, mix_ref, *, heads):
    block = pl.program_id(0)
    rows = query_ref.shape[0]
    width = query_ref.shape[1]
    keys_per_block = key_ref.shape[0]
    first = first_ref[0]

    @pl.when(block == 0)
    def _():
        top_ref[...] = jnp.full(top_ref.shape, very_negative, jnp.float32)
        total_ref[...] = jnp.zeros(total_ref.shape, jnp.float32)
        mix_ref[...] = jnp.zeros(mix_ref.shape, jnp.float32)

    def accumulate(masked):
        scores = lax.dot_general(
            query_ref[...], key_ref[...], (((1,), (1,)), ((), ())), preferred_element_type=jnp.float32
        ) * (1.0 / math.sqrt(width))
        if masked:
            row = lax.broadcasted_iota(jnp.int32, scores.shape, 0)
            col = lax.broadcasted_iota(jnp.int32, scores.shape, 1)
            allowed = block * keys_per_block + col <= first + row // heads
            scores = jnp.where(allowed, scores, very_negative)
        top_old = top_ref[...]
        top_new = jnp.maximum(top_old, jnp.max(scores, axis=1, keepdims=True))
        rescale = jnp.exp(top_old - top_new)
        weights = jnp.exp(scores - top_new)
        if masked:
            weights = jnp.where(allowed, weights, 0.0)
        total_ref[...] = rescale * total_ref[...] + jnp.sum(weights, axis=1, keepdims=True)
        weights_hi = weights.astype(jnp.bfloat16)
        weights_lo = (weights - weights_hi.astype(jnp.float32)).astype(jnp.bfloat16)
        upper = upper_ref[...]
        mixed = (
            jnp.dot(weights_hi, upper, preferred_element_type=jnp.float32)
            + jnp.dot(weights_hi, lower_ref[...], preferred_element_type=jnp.float32)
            + jnp.dot(weights_lo, upper, preferred_element_type=jnp.float32)
        )
        mix_ref[...] = rescale * mix_ref[...] + mixed
        top_ref[...] = top_new

    block_end = (block + 1) * keys_per_block - 1

    @pl.when(block_end <= first)
    def _():
        accumulate(False)

    @pl.when(jnp.logical_and(block_end > first, block * keys_per_block <= first + rows // heads - 1))
    def _():
        accumulate(True)

    @pl.when(block == pl.num_programs(0) - 1)
    def _():
        out_ref[...] = mix_ref[...] / total_ref[...]


def attend(first_query, query_rows, every, heads, keys_per_block=512):
    rows, width = query_rows.shape
    blocks = every.shape[0] // keys_per_block
    flops = 2 * rows * every.shape[0] * width * 4
    return pl.pallas_call(
        functools.partial(attend_kernel, heads=heads),
        out_shape=jax.ShapeDtypeStruct((rows, width), jnp.float32),
        grid_spec=pltpu.PrefetchScalarGridSpec(
            num_scalar_prefetch=1,
            grid=(blocks,),
            in_specs=[
                pl.BlockSpec((rows, width), lambda b, f: (0, 0)),
                pl.BlockSpec((keys_per_block, width), lambda b, f: (b, 0)),
                pl.BlockSpec((keys_per_block, width), lambda b, f: (b, 1)),
                pl.BlockSpec((keys_per_block, width), lambda b, f: (b, 2)),
            ],
            out_specs=pl.BlockSpec((rows, width), lambda b, f: (0, 0)),
            scratch_shapes=[
                pltpu.VMEM((rows, 1), jnp.float32),
                pltpu.VMEM((rows, 1), jnp.float32),
                pltpu.VMEM((rows, width), jnp.float32),
            ],
        ),
        compiler_params=pltpu.CompilerParams(dimension_semantics=("arbitrary",)),
        cost_estimate=pl.CostEstimate(
            flops=flops,
            transcendentals=rows * every.shape[0],
            bytes_accessed=every.size * 2 + query_rows.size * 2 + rows * width * 4,
        ),
    )(first_query, query_rows, every, every, every)


def local(queries, keys, values, inputs_x, in_b, in_c, log_decay):
    row_count = queries.shape[0]
    heads = queries.shape[1] // HEAD_WIDTH
    seq_count = lax.axis_size("seq")
    own_index = lax.axis_index("seq")
    first_query = own_index * row_count

    values_hi, values_lo = split_bf16(values)
    packed = jnp.concatenate([keys, values_hi, values_lo], axis=1)

    c_scale = 0.5 / math.sqrt(N * row_count * seq_count)
    student_x = inputs_x.astype(jnp.float32).reshape(row_count, heads, HEAD_WIDTH)
    b_rows = in_b.astype(jnp.float32)
    c_rows = in_c.astype(jnp.float32) * c_scale
    cumulative = jnp.cumsum(log_decay, axis=0)
    totals = cumulative[-1]
    heads_first = cumulative.T
    causal = jnp.arange(row_count)[:, None] >= jnp.arange(row_count)[None, :]
    decays = jnp.exp(
        jnp.where(causal[None], heads_first[:, :, None] - heads_first[:, None, :], -jnp.inf)
    )
    inner_products = jnp.dot(in_c, in_b.T, preferred_element_type=jnp.float32) * c_scale
    mixing = decays * inner_products[None]
    rising = jnp.exp(cumulative)
    ending = jnp.exp(totals[None, :] - cumulative)
    local_state = jnp.einsum(
        "shp,sn->hpn", student_x * ending[:, :, None], b_rows, precision=highest
    )
    state_in, plane_blocks = exclusive_scan(local_state, totals, "seq", True, packed)
    every = gather_groups(plane_blocks, "seq")

    query_rows = queries.reshape(row_count * heads, HEAD_WIDTH)
    teacher_out = attend(
        jnp.reshape(first_query, (1,)).astype(jnp.int32), query_rows, every, heads
    ).reshape(row_count, heads, HEAD_WIDTH)

    y_intra = jnp.einsum("hts,shp->thp", mixing, student_x, precision=highest)
    y_inter = jnp.einsum("tn,hpn->thp", c_rows, state_in, precision=highest) * rising[:, :, None]
    mismatch = y_intra + y_inter - teacher_out
    scaled_mismatch = mismatch * rising[:, :, None]
    local_grad = jnp.einsum("thp,tn->hpn", scaled_mismatch, c_rows, precision=highest)
    later_grad, _ = exclusive_scan(local_grad, totals, "seq", False)
    grad_x = jnp.einsum("hts,thp->shp", mixing, mismatch, precision=highest)
    grad_x = (
        grad_x
        + jnp.einsum("hpn,sn->shp", later_grad, b_rows, precision=highest) * ending[:, :, None]
    )
    products = jnp.einsum("thp,shp->hts", mismatch, student_x, precision=highest)
    weighted = decays * products
    grad_b = jnp.einsum("hts,tn->sn", weighted, c_rows, precision=highest)
    grad_b = grad_b + jnp.einsum(
        "shp,hpn->sn", student_x * ending[:, :, None], later_grad, precision=highest
    )
    grad_c = jnp.einsum("hts,sn->tn", weighted, b_rows, precision=highest)
    grad_c = grad_c + jnp.einsum("thp,hpn->tn", scaled_mismatch, state_in, precision=highest)
    summed = mp_sum_scatter(jnp.concatenate([grad_b, grad_c], axis=1), "mp")
    summed_b, summed_c = summed[:, :N], summed[:, N:]
    return (grad_x.reshape(row_count, heads * HEAD_WIDTH), summed_b, summed_c * c_scale)


def solution(mesh):
    in_specs = (
        P("seq", "mp"),
        P("seq", "mp"),
        P("seq", "mp"),
        P("seq", "mp"),
        P("seq", None),
        P("seq", None),
        P("seq", "mp"),
    )
    out_specs = (P("seq", "mp"), P(("seq", "mp"), None), P(("seq", "mp"), None))
    return jax.shard_map(local, mesh=mesh, in_specs=in_specs, out_specs=out_specs, check_vma=False)
```

```python
import functools
import math

import jax
import jax.numpy as jnp
from jax import lax
from jax.experimental import pallas as pl
from jax.experimental.pallas import tpu as pltpu
from jax.sharding import PartitionSpec as P

HEAD_WIDTH = 128
N = 128

very_negative = -1e30
highest = lax.Precision.HIGHEST


def shift(value, axis, distance, forward):
    count = lax.axis_size(axis)
    if forward:
        perm = [(j, j + distance) for j in range(count - distance)]
    else:
        perm = [(j + distance, j) for j in range(count - distance)]
    return lax.ppermute(value, axis, perm)


def send_with_logs(state, logs, axis, perm, extra=None):
    heads, rows, width = state.shape
    count = logs.shape[0]
    log_rows = jnp.pad(jnp.broadcast_to(logs[:, None], (count, width)), ((0, -count % 8), (0, 0)))
    payload = jnp.concatenate([state.reshape(heads * rows, width), log_rows], axis=0)
    if extra is None:
        got = lax.ppermute(payload, axis, perm)
        got_extra = None
    else:
        got, got_extra = lax.ppermute((payload, extra), axis, perm)
    got_state = got[: heads * rows].reshape(heads, rows, width)
    got_logs = got[heads * rows : heads * rows + count, 0]
    if extra is None:
        return got_state, got_logs
    return got_state, got_logs, got_extra


def shift_perm(count, distance, forward):
    if forward:
        return [(j, j + distance) for j in range(count - distance)]
    return [(j + distance, j) for j in range(count - distance)]


def pair_down(state, logs, axis, bit, forward, extra=None):
    count = lax.axis_size(axis)
    upper = (lax.axis_index(axis) // bit) % 2 == 1
    first = jnp.logical_not(upper) if forward else upper
    half = state.shape[0] // 2
    mine = jnp.where(upper, half, 0)
    other = half - mine
    own_state = lax.dynamic_slice_in_dim(state, mine, half, axis=0)
    own_logs = lax.dynamic_slice_in_dim(logs, mine, half)
    sent = send_with_logs(
        lax.dynamic_slice_in_dim(state, other, half, axis=0),
        lax.dynamic_slice_in_dim(logs, other, half),
        axis,
        [(j, j ^ bit) for j in range(count)],
        extra,
    )
    got_state, got_logs = sent[:2]
    joined = None
    if extra is not None:
        joined = sent[2]
        joined = jnp.where(
            upper, jnp.concatenate([joined, extra], axis=0), jnp.concatenate([extra, joined], axis=0)
        )
    first_state = jnp.where(first, own_state, got_state)
    second_state = jnp.where(first, got_state, own_state)
    first_logs = jnp.where(first, own_logs, got_logs)
    second_logs = jnp.where(first, got_logs, own_logs)
    pair_state = jnp.exp(second_logs)[:, None, None] * first_state + second_state
    return pair_state, first_logs + second_logs, (first_state, first_logs), joined


def pair_up(window, saved, axis, bit, forward):
    count = lax.axis_size(axis)
    upper = (lax.axis_index(axis) // bit) % 2 == 1
    first = jnp.logical_not(upper) if forward else upper
    first_state, first_logs = saved
    second_window = jnp.exp(first_logs)[:, None, None] * window + first_state
    keep = jnp.where(first, window, second_window)
    send = jnp.where(first, second_window, window)
    got = lax.ppermute(send, axis, [(j, j ^ bit) for j in range(count)])
    return jnp.where(
        upper, jnp.concatenate([got, keep], axis=0), jnp.concatenate([keep, got], axis=0)
    )


def exclusive_scan(state, logs, axis, forward, extra=None):
    count = lax.axis_size(axis)
    levels = []
    for bit in (1, 2):
        state, logs, saved, extra = pair_down(state, logs, axis, bit, forward, extra)
        levels.append((bit, saved))
    stride = 4
    groups = count // stride
    window_state, window_log = send_with_logs(state, logs, axis, shift_perm(count, stride, forward))
    width = 1
    while width < groups:
        perm = shift_perm(count, stride * width, forward)
        if width * 2 < groups:
            got_state, got_log = send_with_logs(window_state, window_log, axis, perm)
            window_log_next = window_log + got_log
        else:
            got_state = lax.ppermute(window_state, axis, perm)
            window_log_next = window_log
        window_state = window_state + jnp.exp(window_log)[:, None, None] * got_state
        window_log = window_log_next
        width *= 2
    for bit, saved in reversed(levels):
        window_state = pair_up(window_state, saved, axis, bit, forward)
    return window_state, extra


def gather_groups(pieces, axis):
    count = lax.axis_size(axis)
    groups = [[z * 4 + r for z in range(count // 4)] for r in range(4)]
    return lax.all_gather(pieces, axis, axis=0, tiled=True, axis_index_groups=groups)


def split_bf16(value):
    upper = lax.reduce_precision(value, exponent_bits=8, mantissa_bits=7)
    return upper.astype(jnp.bfloat16), (value - upper).astype(jnp.bfloat16)


def mp_sum_scatter(value, axis):
    count = lax.axis_size(axis)
    blocks = value.reshape(count, value.shape[0] // count, value.shape[1])
    return jnp.sum(lax.all_to_all(blocks, axis, 0, 0), axis=0)


def attend_kernel(first_ref, query_ref, key_ref, upper_ref, lower_ref, out_ref, top_ref, total_ref, mix_ref, *, heads):
    block = pl.program_id(0)
    rows = query_ref.shape[0]
    width = query_ref.shape[1]
    keys_per_block = key_ref.shape[0]
    first = first_ref[0]

    @pl.when(block == 0)
    def _():
        top_ref[...] = jnp.full(top_ref.shape, very_negative, jnp.float32)
        total_ref[...] = jnp.zeros(total_ref.shape, jnp.float32)
        mix_ref[...] = jnp.zeros(mix_ref.shape, jnp.float32)

    def accumulate(masked):
        scores = lax.dot_general(
            query_ref[...], key_ref[...], (((1,), (1,)), ((), ())), preferred_element_type=jnp.float32
        ) * (1.0 / math.sqrt(width))
        if masked:
            row = lax.broadcasted_iota(jnp.int32, scores.shape, 0)
            col = lax.broadcasted_iota(jnp.int32, scores.shape, 1)
            allowed = block * keys_per_block + col <= first + row // heads
            scores = jnp.where(allowed, scores, very_negative)
        top_old = top_ref[...]
        top_new = jnp.maximum(top_old, jnp.max(scores, axis=1, keepdims=True))
        rescale = jnp.exp(top_old - top_new)
        weights = jnp.exp(scores - top_new)
        if masked:
            weights = jnp.where(allowed, weights, 0.0)
        total_ref[...] = rescale * total_ref[...] + jnp.sum(weights, axis=1, keepdims=True)
        weights_hi = weights.astype(jnp.bfloat16)
        weights_lo = (weights - weights_hi.astype(jnp.float32)).astype(jnp.bfloat16)
        upper = upper_ref[...]
        mixed = (
            jnp.dot(weights_hi, upper, preferred_element_type=jnp.float32)
            + jnp.dot(weights_hi, lower_ref[...], preferred_element_type=jnp.float32)
            + jnp.dot(weights_lo, upper, preferred_element_type=jnp.float32)
        )
        mix_ref[...] = rescale * mix_ref[...] + mixed
        top_ref[...] = top_new

    block_end = (block + 1) * keys_per_block - 1

    @pl.when(block_end <= first)
    def _():
        accumulate(False)

    @pl.when(jnp.logical_and(block_end > first, block * keys_per_block <= first + rows // heads - 1))
    def _():
        accumulate(True)

    @pl.when(block == pl.num_programs(0) - 1)
    def _():
        out_ref[...] = mix_ref[...] / total_ref[...]


def attend(first_query, query_rows, every, heads, keys_per_block=1024):
    rows, width = query_rows.shape
    blocks = every.shape[0] // keys_per_block
    flops = 2 * rows * every.shape[0] * width * 4
    return pl.pallas_call(
        functools.partial(attend_kernel, heads=heads),
        out_shape=jax.ShapeDtypeStruct((rows, width), jnp.float32),
        grid_spec=pltpu.PrefetchScalarGridSpec(
            num_scalar_prefetch=1,
            grid=(blocks,),
            in_specs=[
                pl.BlockSpec((rows, width), lambda b, f: (0, 0)),
                pl.BlockSpec((keys_per_block, width), lambda b, f: (b, 0)),
                pl.BlockSpec((keys_per_block, width), lambda b, f: (b, 1)),
                pl.BlockSpec((keys_per_block, width), lambda b, f: (b, 2)),
            ],
            out_specs=pl.BlockSpec((rows, width), lambda b, f: (0, 0)),
            scratch_shapes=[
                pltpu.VMEM((rows, 1), jnp.float32),
                pltpu.VMEM((rows, 1), jnp.float32),
                pltpu.VMEM((rows, width), jnp.float32),
            ],
        ),
        compiler_params=pltpu.CompilerParams(dimension_semantics=("arbitrary",)),
        cost_estimate=pl.CostEstimate(
            flops=flops,
            transcendentals=rows * every.shape[0],
            bytes_accessed=every.size * 2 + query_rows.size * 2 + rows * width * 4,
        ),
    )(first_query, query_rows, every, every, every)


def local(queries, keys, values, inputs_x, in_b, in_c, log_decay):
    row_count = queries.shape[0]
    heads = queries.shape[1] // HEAD_WIDTH
    seq_count = lax.axis_size("seq")
    own_index = lax.axis_index("seq")
    first_query = own_index * row_count

    values_hi, values_lo = split_bf16(values)
    packed = jnp.concatenate([keys, values_hi, values_lo], axis=1)

    c_scale = 0.5 / math.sqrt(N * row_count * seq_count)
    student_x = inputs_x.astype(jnp.float32).reshape(row_count, heads, HEAD_WIDTH)
    b_rows = in_b.astype(jnp.float32)
    c_rows = in_c.astype(jnp.float32) * c_scale
    cumulative = jnp.cumsum(log_decay, axis=0)
    totals = cumulative[-1]
    heads_first = cumulative.T
    causal = jnp.arange(row_count)[:, None] >= jnp.arange(row_count)[None, :]
    decays = jnp.exp(
        jnp.where(causal[None], heads_first[:, :, None] - heads_first[:, None, :], -jnp.inf)
    )
    inner_products = jnp.dot(in_c, in_b.T, preferred_element_type=jnp.float32) * c_scale
    mixing = decays * inner_products[None]
    rising = jnp.exp(cumulative)
    ending = jnp.exp(totals[None, :] - cumulative)
    local_state = jnp.einsum(
        "shp,sn->hpn", student_x * ending[:, :, None], b_rows, precision=highest
    )
    state_in, plane_blocks = exclusive_scan(local_state, totals, "seq", True, packed)
    every = gather_groups(plane_blocks, "seq")

    query_rows = queries.reshape(row_count * heads, HEAD_WIDTH)
    teacher_out = attend(
        jnp.reshape(first_query, (1,)).astype(jnp.int32), query_rows, every, heads
    ).reshape(row_count, heads, HEAD_WIDTH)

    y_intra = jnp.einsum("hts,shp->thp", mixing, student_x, precision=highest)
    y_inter = jnp.einsum("tn,hpn->thp", c_rows, state_in, precision=highest) * rising[:, :, None]
    mismatch = y_intra + y_inter - teacher_out
    scaled_mismatch = mismatch * rising[:, :, None]
    local_grad = jnp.einsum("thp,tn->hpn", scaled_mismatch, c_rows, precision=highest)
    later_grad, _ = exclusive_scan(local_grad, totals, "seq", False)
    grad_x = jnp.einsum("hts,thp->shp", mixing, mismatch, precision=highest)
    grad_x = (
        grad_x
        + jnp.einsum("hpn,sn->shp", later_grad, b_rows, precision=highest) * ending[:, :, None]
    )
    products = jnp.einsum("thp,shp->hts", mismatch, student_x, precision=highest)
    weighted = decays * products
    grad_b = jnp.einsum("hts,tn->sn", weighted, c_rows, precision=highest)
    grad_b = grad_b + jnp.einsum(
        "shp,hpn->sn", student_x * ending[:, :, None], later_grad, precision=highest
    )
    grad_c = jnp.einsum("hts,sn->tn", weighted, b_rows, precision=highest)
    grad_c = grad_c + jnp.einsum("thp,hpn->tn", scaled_mismatch, state_in, precision=highest)
    summed = mp_sum_scatter(jnp.concatenate([grad_b, grad_c], axis=1), "mp")
    summed_b, summed_c = summed[:, :N], summed[:, N:]
    return (grad_x.reshape(row_count, heads * HEAD_WIDTH), summed_b, summed_c * c_scale)


def solution(mesh):
    in_specs = (
        P("seq", "mp"),
        P("seq", "mp"),
        P("seq", "mp"),
        P("seq", "mp"),
        P("seq", None),
        P("seq", None),
        P("seq", "mp"),
    )
    out_specs = (P("seq", "mp"), P(("seq", "mp"), None), P(("seq", "mp"), None))
    return jax.shard_map(local, mesh=mesh, in_specs=in_specs, out_specs=out_specs, check_vma=False)
```

```python
import functools
import math

import jax
import jax.numpy as jnp
from jax import lax
from jax.experimental import pallas as pl
from jax.experimental.pallas import tpu as pltpu
from jax.sharding import PartitionSpec as P

HEAD_WIDTH = 128
N = 128

very_negative = -1e30
highest = lax.Precision.HIGHEST


def shift(value, axis, distance, forward):
    count = lax.axis_size(axis)
    if forward:
        perm = [(j, j + distance) for j in range(count - distance)]
    else:
        perm = [(j + distance, j) for j in range(count - distance)]
    return lax.ppermute(value, axis, perm)


def send_with_logs(state, logs, axis, perm, extra=None):
    heads, rows, width = state.shape
    count = logs.shape[0]
    log_rows = jnp.pad(jnp.broadcast_to(logs[:, None], (count, width)), ((0, -count % 8), (0, 0)))
    payload = jnp.concatenate([state.reshape(heads * rows, width), log_rows], axis=0)
    if extra is None:
        got = lax.ppermute(payload, axis, perm)
        got_extra = None
    else:
        got, got_extra = lax.ppermute((payload, extra), axis, perm)
    got_state = got[: heads * rows].reshape(heads, rows, width)
    got_logs = got[heads * rows : heads * rows + count, 0]
    if extra is None:
        return got_state, got_logs
    return got_state, got_logs, got_extra


def shift_perm(count, distance, forward):
    if forward:
        return [(j, j + distance) for j in range(count - distance)]
    return [(j + distance, j) for j in range(count - distance)]


def pair_down(state, logs, axis, bit, forward, extra=None):
    count = lax.axis_size(axis)
    upper = (lax.axis_index(axis) // bit) % 2 == 1
    first = jnp.logical_not(upper) if forward else upper
    half = state.shape[0] // 2
    mine = jnp.where(upper, half, 0)
    other = half - mine
    own_state = lax.dynamic_slice_in_dim(state, mine, half, axis=0)
    own_logs = lax.dynamic_slice_in_dim(logs, mine, half)
    sent = send_with_logs(
        lax.dynamic_slice_in_dim(state, other, half, axis=0),
        lax.dynamic_slice_in_dim(logs, other, half),
        axis,
        [(j, j ^ bit) for j in range(count)],
        extra,
    )
    got_state, got_logs = sent[:2]
    joined = None
    if extra is not None:
        joined = sent[2]
        joined = jnp.where(
            upper, jnp.concatenate([joined, extra], axis=0), jnp.concatenate([extra, joined], axis=0)
        )
    first_state = jnp.where(first, own_state, got_state)
    second_state = jnp.where(first, got_state, own_state)
    first_logs = jnp.where(first, own_logs, got_logs)
    second_logs = jnp.where(first, got_logs, own_logs)
    pair_state = jnp.exp(second_logs)[:, None, None] * first_state + second_state
    return pair_state, first_logs + second_logs, (first_state, first_logs), joined


def pair_up(window, saved, axis, bit, forward):
    count = lax.axis_size(axis)
    upper = (lax.axis_index(axis) // bit) % 2 == 1
    first = jnp.logical_not(upper) if forward else upper
    first_state, first_logs = saved
    second_window = jnp.exp(first_logs)[:, None, None] * window + first_state
    keep = jnp.where(first, window, second_window)
    send = jnp.where(first, second_window, window)
    got = lax.ppermute(send, axis, [(j, j ^ bit) for j in range(count)])
    return jnp.where(
        upper, jnp.concatenate([got, keep], axis=0), jnp.concatenate([keep, got], axis=0)
    )


def exclusive_scan(state, logs, axis, forward, extra=None):
    count = lax.axis_size(axis)
    levels = []
    for bit in (1, 2):
        state, logs, saved, extra = pair_down(state, logs, axis, bit, forward, extra)
        levels.append((bit, saved))
    stride = 4
    groups = count // stride
    window_state, window_log = send_with_logs(state, logs, axis, shift_perm(count, stride, forward))
    width = 1
    while width < groups:
        perm = shift_perm(count, stride * width, forward)
        if width * 2 < groups:
            got_state, got_log = send_with_logs(window_state, window_log, axis, perm)
            window_log_next = window_log + got_log
        else:
            got_state = lax.ppermute(window_state, axis, perm)
            window_log_next = window_log
        window_state = window_state + jnp.exp(window_log)[:, None, None] * got_state
        window_log = window_log_next
        width *= 2
    for bit, saved in reversed(levels):
        window_state = pair_up(window_state, saved, axis, bit, forward)
    return window_state, extra


def gather_groups(pieces, axis):
    count = lax.axis_size(axis)
    groups = [[z * 4 + r for z in range(count // 4)] for r in range(4)]
    return lax.all_gather(pieces, axis, axis=0, tiled=True, axis_index_groups=groups)


def split_bf16(value):
    upper = lax.reduce_precision(value, exponent_bits=8, mantissa_bits=7)
    return upper.astype(jnp.bfloat16), (value - upper).astype(jnp.bfloat16)


def mp_sum_scatter(value, axis):
    count = lax.axis_size(axis)
    blocks = value.reshape(count, value.shape[0] // count, value.shape[1])
    return jnp.sum(lax.all_to_all(blocks, axis, 0, 0), axis=0)


def attend_kernel(first_ref, query_ref, key_ref, upper_ref, lower_ref, out_ref, top_ref, total_ref, mix_ref, *, heads):
    block = pl.program_id(0)
    rows = query_ref.shape[0]
    width = query_ref.shape[1]
    keys_per_block = key_ref.shape[0]
    first = first_ref[0]

    @pl.when(block == 0)
    def _():
        top_ref[...] = jnp.full(top_ref.shape, very_negative, jnp.float32)
        total_ref[...] = jnp.zeros(total_ref.shape, jnp.float32)
        mix_ref[...] = jnp.zeros(mix_ref.shape, jnp.float32)

    def accumulate(masked):
        scores = lax.dot_general(
            query_ref[...], key_ref[...], (((1,), (1,)), ((), ())), preferred_element_type=jnp.float32
        ) * (1.0 / math.sqrt(width))
        if masked:
            row = lax.broadcasted_iota(jnp.int32, scores.shape, 0)
            col = lax.broadcasted_iota(jnp.int32, scores.shape, 1)
            allowed = block * keys_per_block + col <= first + row // heads
            scores = jnp.where(allowed, scores, very_negative)
        top_old = top_ref[...]
        top_new = jnp.maximum(top_old, jnp.max(scores, axis=1, keepdims=True))
        rescale = jnp.exp(top_old - top_new)
        weights = jnp.exp(scores - top_new)
        if masked:
            weights = jnp.where(allowed, weights, 0.0)
        total_ref[...] = rescale * total_ref[...] + jnp.sum(weights, axis=1, keepdims=True)
        value_rows = upper_ref[...].astype(jnp.float32) + lower_ref[...].astype(jnp.float32)
        mixed = jnp.dot(
            weights, value_rows, precision=lax.Precision.HIGHEST, preferred_element_type=jnp.float32
        )
        mix_ref[...] = rescale * mix_ref[...] + mixed
        top_ref[...] = top_new

    block_end = (block + 1) * keys_per_block - 1

    @pl.when(block_end <= first)
    def _():
        accumulate(False)

    @pl.when(jnp.logical_and(block_end > first, block * keys_per_block <= first + rows // heads - 1))
    def _():
        accumulate(True)

    @pl.when(block == pl.num_programs(0) - 1)
    def _():
        out_ref[...] = mix_ref[...] / total_ref[...]


def attend(first_query, query_rows, every, heads, keys_per_block=512):
    rows, width = query_rows.shape
    blocks = every.shape[0] // keys_per_block
    flops = 2 * rows * every.shape[0] * width * 4
    return pl.pallas_call(
        functools.partial(attend_kernel, heads=heads),
        out_shape=jax.ShapeDtypeStruct((rows, width), jnp.float32),
        grid_spec=pltpu.PrefetchScalarGridSpec(
            num_scalar_prefetch=1,
            grid=(blocks,),
            in_specs=[
                pl.BlockSpec((rows, width), lambda b, f: (0, 0)),
                pl.BlockSpec((keys_per_block, width), lambda b, f: (b, 0)),
                pl.BlockSpec((keys_per_block, width), lambda b, f: (b, 1)),
                pl.BlockSpec((keys_per_block, width), lambda b, f: (b, 2)),
            ],
            out_specs=pl.BlockSpec((rows, width), lambda b, f: (0, 0)),
            scratch_shapes=[
                pltpu.VMEM((rows, 1), jnp.float32),
                pltpu.VMEM((rows, 1), jnp.float32),
                pltpu.VMEM((rows, width), jnp.float32),
            ],
        ),
        compiler_params=pltpu.CompilerParams(dimension_semantics=("arbitrary",)),
        cost_estimate=pl.CostEstimate(
            flops=flops,
            transcendentals=rows * every.shape[0],
            bytes_accessed=every.size * 2 + query_rows.size * 2 + rows * width * 4,
        ),
    )(first_query, query_rows, every, every, every)


def local(queries, keys, values, inputs_x, in_b, in_c, log_decay):
    row_count = queries.shape[0]
    heads = queries.shape[1] // HEAD_WIDTH
    seq_count = lax.axis_size("seq")
    own_index = lax.axis_index("seq")
    first_query = own_index * row_count

    values_hi, values_lo = split_bf16(values)
    packed = jnp.concatenate([keys, values_hi, values_lo], axis=1)

    c_scale = 0.5 / math.sqrt(N * row_count * seq_count)
    student_x = inputs_x.astype(jnp.float32).reshape(row_count, heads, HEAD_WIDTH)
    b_rows = in_b.astype(jnp.float32)
    c_rows = in_c.astype(jnp.float32) * c_scale
    cumulative = jnp.cumsum(log_decay, axis=0)
    totals = cumulative[-1]
    heads_first = cumulative.T
    causal = jnp.arange(row_count)[:, None] >= jnp.arange(row_count)[None, :]
    decays = jnp.exp(
        jnp.where(causal[None], heads_first[:, :, None] - heads_first[:, None, :], -jnp.inf)
    )
    inner_products = jnp.dot(in_c, in_b.T, preferred_element_type=jnp.float32) * c_scale
    mixing = decays * inner_products[None]
    rising = jnp.exp(cumulative)
    ending = jnp.exp(totals[None, :] - cumulative)
    local_state = jnp.einsum(
        "shp,sn->hpn", student_x * ending[:, :, None], b_rows, precision=highest
    )
    state_in, plane_blocks = exclusive_scan(local_state, totals, "seq", True, packed)
    every = gather_groups(plane_blocks, "seq")

    query_rows = queries.reshape(row_count * heads, HEAD_WIDTH)
    teacher_out = attend(
        jnp.reshape(first_query, (1,)).astype(jnp.int32), query_rows, every, heads
    ).reshape(row_count, heads, HEAD_WIDTH)

    y_intra = jnp.einsum("hts,shp->thp", mixing, student_x, precision=highest)
    y_inter = jnp.einsum("tn,hpn->thp", c_rows, state_in, precision=highest) * rising[:, :, None]
    mismatch = y_intra + y_inter - teacher_out
    scaled_mismatch = mismatch * rising[:, :, None]
    local_grad = jnp.einsum("thp,tn->hpn", scaled_mismatch, c_rows, precision=highest)
    later_grad, _ = exclusive_scan(local_grad, totals, "seq", False)
    grad_x = jnp.einsum("hts,thp->shp", mixing, mismatch, precision=highest)
    grad_x = (
        grad_x
        + jnp.einsum("hpn,sn->shp", later_grad, b_rows, precision=highest) * ending[:, :, None]
    )
    products = jnp.einsum("thp,shp->hts", mismatch, student_x, precision=highest)
    weighted = decays * products
    grad_b = jnp.einsum("hts,tn->sn", weighted, c_rows, precision=highest)
    grad_b = grad_b + jnp.einsum(
        "shp,hpn->sn", student_x * ending[:, :, None], later_grad, precision=highest
    )
    grad_c = jnp.einsum("hts,sn->tn", weighted, b_rows, precision=highest)
    grad_c = grad_c + jnp.einsum("thp,hpn->tn", scaled_mismatch, state_in, precision=highest)
    summed = mp_sum_scatter(jnp.concatenate([grad_b, grad_c], axis=1), "mp")
    summed_b, summed_c = summed[:, :N], summed[:, N:]
    return (grad_x.reshape(row_count, heads * HEAD_WIDTH), summed_b, summed_c * c_scale)


def solution(mesh):
    in_specs = (
        P("seq", "mp"),
        P("seq", "mp"),
        P("seq", "mp"),
        P("seq", "mp"),
        P("seq", None),
        P("seq", None),
        P("seq", "mp"),
    )
    out_specs = (P("seq", "mp"), P(("seq", "mp"), None), P(("seq", "mp"), None))
    return jax.shard_map(local, mesh=mesh, in_specs=in_specs, out_specs=out_specs, check_vma=False)
```

```python
import functools
import math

import jax
import jax.numpy as jnp
from jax import lax
from jax.experimental import pallas as pl
from jax.experimental.pallas import tpu as pltpu
from jax.sharding import PartitionSpec as P

HEAD_WIDTH = 128
N = 128

very_negative = -1e30
highest = lax.Precision.HIGHEST


def shift(value, axis, distance, forward):
    count = lax.axis_size(axis)
    if forward:
        perm = [(j, j + distance) for j in range(count - distance)]
    else:
        perm = [(j + distance, j) for j in range(count - distance)]
    return lax.ppermute(value, axis, perm)


def send_with_logs(state, logs, axis, perm, extra=None):
    heads, rows, width = state.shape
    count = logs.shape[0]
    log_rows = jnp.pad(jnp.broadcast_to(logs[:, None], (count, width)), ((0, -count % 8), (0, 0)))
    payload = jnp.concatenate([state.reshape(heads * rows, width), log_rows], axis=0)
    if extra is None:
        got = lax.ppermute(payload, axis, perm)
        got_extra = None
    else:
        got, got_extra = lax.ppermute((payload, extra), axis, perm)
    got_state = got[: heads * rows].reshape(heads, rows, width)
    got_logs = got[heads * rows : heads * rows + count, 0]
    if extra is None:
        return got_state, got_logs
    return got_state, got_logs, got_extra


def shift_perm(count, distance, forward):
    if forward:
        return [(j, j + distance) for j in range(count - distance)]
    return [(j + distance, j) for j in range(count - distance)]


def pair_down(state, logs, axis, bit, forward, extra=None):
    count = lax.axis_size(axis)
    upper = (lax.axis_index(axis) // bit) % 2 == 1
    first = jnp.logical_not(upper) if forward else upper
    half = state.shape[0] // 2
    mine = jnp.where(upper, half, 0)
    other = half - mine
    own_state = lax.dynamic_slice_in_dim(state, mine, half, axis=0)
    own_logs = lax.dynamic_slice_in_dim(logs, mine, half)
    sent = send_with_logs(
        lax.dynamic_slice_in_dim(state, other, half, axis=0),
        lax.dynamic_slice_in_dim(logs, other, half),
        axis,
        [(j, j ^ bit) for j in range(count)],
        extra,
    )
    got_state, got_logs = sent[:2]
    joined = None
    if extra is not None:
        joined = sent[2]
        joined = jnp.where(
            upper, jnp.concatenate([joined, extra], axis=0), jnp.concatenate([extra, joined], axis=0)
        )
    first_state = jnp.where(first, own_state, got_state)
    second_state = jnp.where(first, got_state, own_state)
    first_logs = jnp.where(first, own_logs, got_logs)
    second_logs = jnp.where(first, got_logs, own_logs)
    pair_state = jnp.exp(second_logs)[:, None, None] * first_state + second_state
    return pair_state, first_logs + second_logs, (first_state, first_logs), joined


def pair_up(window, saved, axis, bit, forward):
    count = lax.axis_size(axis)
    upper = (lax.axis_index(axis) // bit) % 2 == 1
    first = jnp.logical_not(upper) if forward else upper
    first_state, first_logs = saved
    second_window = jnp.exp(first_logs)[:, None, None] * window + first_state
    keep = jnp.where(first, window, second_window)
    send = jnp.where(first, second_window, window)
    got = lax.ppermute(send, axis, [(j, j ^ bit) for j in range(count)])
    return jnp.where(
        upper, jnp.concatenate([got, keep], axis=0), jnp.concatenate([keep, got], axis=0)
    )


def exclusive_scan(state, logs, axis, forward, extra=None):
    count = lax.axis_size(axis)
    levels = []
    for bit in (1, 2):
        state, logs, saved, extra = pair_down(state, logs, axis, bit, forward, extra)
        levels.append((bit, saved))
    stride = 4
    groups = count // stride
    window_state, window_log = send_with_logs(state, logs, axis, shift_perm(count, stride, forward))
    width = 1
    while width < groups:
        perm = shift_perm(count, stride * width, forward)
        if width * 2 < groups:
            got_state, got_log = send_with_logs(window_state, window_log, axis, perm)
            window_log_next = window_log + got_log
        else:
            got_state = lax.ppermute(window_state, axis, perm)
            window_log_next = window_log
        window_state = window_state + jnp.exp(window_log)[:, None, None] * got_state
        window_log = window_log_next
        width *= 2
    for bit, saved in reversed(levels):
        window_state = pair_up(window_state, saved, axis, bit, forward)
    return window_state, extra


def gather_groups(pieces, axis):
    count = lax.axis_size(axis)
    groups = [[z * 4 + r for z in range(count // 4)] for r in range(4)]
    return lax.all_gather(pieces, axis, axis=0, tiled=True, axis_index_groups=groups)


def split_bf16(value):
    upper = lax.reduce_precision(value, exponent_bits=8, mantissa_bits=7)
    return upper.astype(jnp.bfloat16), (value - upper).astype(jnp.bfloat16)


def mp_sum_scatter(value, axis):
    count = lax.axis_size(axis)
    blocks = value.reshape(count, value.shape[0] // count, value.shape[1])
    return jnp.sum(lax.all_to_all(blocks, axis, 0, 0), axis=0)


def attend_kernel(first_ref, query_ref, key_ref, upper_ref, lower_ref, out_ref, top_ref, total_ref, mix_ref, *, heads):
    block = pl.program_id(0)
    rows = query_ref.shape[0]
    width = query_ref.shape[1]
    keys_per_block = key_ref.shape[0]
    first = first_ref[0]

    @pl.when(block == 0)
    def _():
        top_ref[...] = jnp.full(top_ref.shape, very_negative, jnp.float32)
        total_ref[...] = jnp.zeros(total_ref.shape, jnp.float32)
        mix_ref[...] = jnp.zeros(mix_ref.shape, jnp.float32)

    def accumulate(masked):
        scores = lax.dot_general(
            query_ref[...], key_ref[...], (((1,), (1,)), ((), ())), preferred_element_type=jnp.float32
        )
        factor = math.log2(math.e) / math.sqrt(width)
        if masked:
            row = lax.broadcasted_iota(jnp.int32, scores.shape, 0)
            col = lax.broadcasted_iota(jnp.int32, scores.shape, 1)
            allowed = block * keys_per_block + col <= first + row // heads
            scores = jnp.where(allowed, scores, very_negative)
        top_old = top_ref[...]
        top_new = jnp.maximum(top_old, jnp.max(scores, axis=1, keepdims=True))
        rescale = jnp.exp2((top_old - top_new) * factor)
        weights = jnp.exp2((scores - top_new) * factor)
        if masked:
            weights = jnp.where(allowed, weights, 0.0)
        total_ref[...] = rescale * total_ref[...] + jnp.sum(weights, axis=1, keepdims=True)
        weights_hi = weights.astype(jnp.bfloat16)
        weights_lo = (weights - weights_hi.astype(jnp.float32)).astype(jnp.bfloat16)
        upper = upper_ref[...]
        mixed = (
            jnp.dot(weights_hi, upper, preferred_element_type=jnp.float32)
            + jnp.dot(weights_hi, lower_ref[...], preferred_element_type=jnp.float32)
            + jnp.dot(weights_lo, upper, preferred_element_type=jnp.float32)
        )
        mix_ref[...] = rescale * mix_ref[...] + mixed
        top_ref[...] = top_new

    block_end = (block + 1) * keys_per_block - 1

    @pl.when(block_end <= first)
    def _():
        accumulate(False)

    @pl.when(jnp.logical_and(block_end > first, block * keys_per_block <= first + rows // heads - 1))
    def _():
        accumulate(True)

    @pl.when(block == pl.num_programs(0) - 1)
    def _():
        out_ref[...] = mix_ref[...] / total_ref[...]


def attend(first_query, query_rows, every, heads, keys_per_block=512):
    rows, width = query_rows.shape
    blocks = every.shape[0] // keys_per_block
    flops = 2 * rows * every.shape[0] * width * 4
    return pl.pallas_call(
        functools.partial(attend_kernel, heads=heads),
        out_shape=jax.ShapeDtypeStruct((rows, width), jnp.float32),
        grid_spec=pltpu.PrefetchScalarGridSpec(
            num_scalar_prefetch=1,
            grid=(blocks,),
            in_specs=[
                pl.BlockSpec((rows, width), lambda b, f: (0, 0)),
                pl.BlockSpec((keys_per_block, width), lambda b, f: (b, 0)),
                pl.BlockSpec((keys_per_block, width), lambda b, f: (b, 1)),
                pl.BlockSpec((keys_per_block, width), lambda b, f: (b, 2)),
            ],
            out_specs=pl.BlockSpec((rows, width), lambda b, f: (0, 0)),
            scratch_shapes=[
                pltpu.VMEM((rows, 1), jnp.float32),
                pltpu.VMEM((rows, 1), jnp.float32),
                pltpu.VMEM((rows, width), jnp.float32),
            ],
        ),
        compiler_params=pltpu.CompilerParams(dimension_semantics=("arbitrary",)),
        cost_estimate=pl.CostEstimate(
            flops=flops,
            transcendentals=rows * every.shape[0],
            bytes_accessed=every.size * 2 + query_rows.size * 2 + rows * width * 4,
        ),
    )(first_query, query_rows, every, every, every)


def local(queries, keys, values, inputs_x, in_b, in_c, log_decay):
    row_count = queries.shape[0]
    heads = queries.shape[1] // HEAD_WIDTH
    seq_count = lax.axis_size("seq")
    own_index = lax.axis_index("seq")
    first_query = own_index * row_count

    values_hi, values_lo = split_bf16(values)
    packed = jnp.concatenate([keys, values_hi, values_lo], axis=1)

    c_scale = 0.5 / math.sqrt(N * row_count * seq_count)
    student_x = inputs_x.astype(jnp.float32).reshape(row_count, heads, HEAD_WIDTH)
    b_rows = in_b.astype(jnp.float32)
    c_rows = in_c.astype(jnp.float32) * c_scale
    cumulative = jnp.cumsum(log_decay, axis=0)
    totals = cumulative[-1]
    heads_first = cumulative.T
    causal = jnp.arange(row_count)[:, None] >= jnp.arange(row_count)[None, :]
    decays = jnp.exp(
        jnp.where(causal[None], heads_first[:, :, None] - heads_first[:, None, :], -jnp.inf)
    )
    inner_products = jnp.dot(in_c, in_b.T, preferred_element_type=jnp.float32) * c_scale
    mixing = decays * inner_products[None]
    rising = jnp.exp(cumulative)
    ending = jnp.exp(totals[None, :] - cumulative)
    local_state = jnp.einsum(
        "shp,sn->hpn", student_x * ending[:, :, None], b_rows, precision=highest
    )
    state_in, plane_blocks = exclusive_scan(local_state, totals, "seq", True, packed)
    every = gather_groups(plane_blocks, "seq")

    query_rows = queries.reshape(row_count * heads, HEAD_WIDTH)
    teacher_out = attend(
        jnp.reshape(first_query, (1,)).astype(jnp.int32), query_rows, every, heads
    ).reshape(row_count, heads, HEAD_WIDTH)

    y_intra = jnp.einsum("hts,shp->thp", mixing, student_x, precision=highest)
    y_inter = jnp.einsum("tn,hpn->thp", c_rows, state_in, precision=highest) * rising[:, :, None]
    mismatch = y_intra + y_inter - teacher_out
    scaled_mismatch = mismatch * rising[:, :, None]
    local_grad = jnp.einsum("thp,tn->hpn", scaled_mismatch, c_rows, precision=highest)
    later_grad, _ = exclusive_scan(local_grad, totals, "seq", False)
    grad_x = jnp.einsum("hts,thp->shp", mixing, mismatch, precision=highest)
    grad_x = (
        grad_x
        + jnp.einsum("hpn,sn->shp", later_grad, b_rows, precision=highest) * ending[:, :, None]
    )
    products = jnp.einsum("thp,shp->hts", mismatch, student_x, precision=highest)
    weighted = decays * products
    grad_b = jnp.einsum("hts,tn->sn", weighted, c_rows, precision=highest)
    grad_b = grad_b + jnp.einsum(
        "shp,hpn->sn", student_x * ending[:, :, None], later_grad, precision=highest
    )
    grad_c = jnp.einsum("hts,sn->tn", weighted, b_rows, precision=highest)
    grad_c = grad_c + jnp.einsum("thp,hpn->tn", scaled_mismatch, state_in, precision=highest)
    summed = mp_sum_scatter(jnp.concatenate([grad_b, grad_c], axis=1), "mp")
    summed_b, summed_c = summed[:, :N], summed[:, N:]
    return (grad_x.reshape(row_count, heads * HEAD_WIDTH), summed_b, summed_c * c_scale)


def solution(mesh):
    in_specs = (
        P("seq", "mp"),
        P("seq", "mp"),
        P("seq", "mp"),
        P("seq", "mp"),
        P("seq", None),
        P("seq", None),
        P("seq", "mp"),
    )
    out_specs = (P("seq", "mp"), P(("seq", "mp"), None), P(("seq", "mp"), None))
    return jax.shard_map(local, mesh=mesh, in_specs=in_specs, out_specs=out_specs, check_vma=False)
```

```python
import functools
import math

import jax
import jax.numpy as jnp
from jax import lax
from jax.experimental import pallas as pl
from jax.experimental.pallas import tpu as pltpu
from jax.sharding import PartitionSpec as P

HEAD_WIDTH = 128
N = 128

very_negative = -1e30
highest = lax.Precision.HIGHEST


def shift(value, axis, distance, forward):
    count = lax.axis_size(axis)
    if forward:
        perm = [(j, j + distance) for j in range(count - distance)]
    else:
        perm = [(j + distance, j) for j in range(count - distance)]
    return lax.ppermute(value, axis, perm)


def send_with_logs(state, logs, axis, perm, extra=None):
    heads, rows, width = state.shape
    count = logs.shape[0]
    log_rows = jnp.pad(jnp.broadcast_to(logs[:, None], (count, width)), ((0, -count % 8), (0, 0)))
    payload = jnp.concatenate([state.reshape(heads * rows, width), log_rows], axis=0)
    if extra is None:
        got = lax.ppermute(payload, axis, perm)
        got_extra = None
    else:
        got, got_extra = lax.ppermute((payload, extra), axis, perm)
    got_state = got[: heads * rows].reshape(heads, rows, width)
    got_logs = got[heads * rows : heads * rows + count, 0]
    if extra is None:
        return got_state, got_logs
    return got_state, got_logs, got_extra


def shift_perm(count, distance, forward):
    if forward:
        return [(j, j + distance) for j in range(count - distance)]
    return [(j + distance, j) for j in range(count - distance)]


def pair_down(state, logs, axis, bit, forward, extra=None):
    count = lax.axis_size(axis)
    upper = (lax.axis_index(axis) // bit) % 2 == 1
    first = jnp.logical_not(upper) if forward else upper
    half = state.shape[0] // 2
    mine = jnp.where(upper, half, 0)
    other = half - mine
    own_state = lax.dynamic_slice_in_dim(state, mine, half, axis=0)
    own_logs = lax.dynamic_slice_in_dim(logs, mine, half)
    sent = send_with_logs(
        lax.dynamic_slice_in_dim(state, other, half, axis=0),
        lax.dynamic_slice_in_dim(logs, other, half),
        axis,
        [(j, j ^ bit) for j in range(count)],
        extra,
    )
    got_state, got_logs = sent[:2]
    joined = None
    if extra is not None:
        joined = sent[2]
        joined = jnp.where(
            upper, jnp.concatenate([joined, extra], axis=0), jnp.concatenate([extra, joined], axis=0)
        )
    first_state = jnp.where(first, own_state, got_state)
    second_state = jnp.where(first, got_state, own_state)
    first_logs = jnp.where(first, own_logs, got_logs)
    second_logs = jnp.where(first, got_logs, own_logs)
    pair_state = jnp.exp(second_logs)[:, None, None] * first_state + second_state
    return pair_state, first_logs + second_logs, (first_state, first_logs), joined


def pair_up(window, saved, axis, bit, forward):
    count = lax.axis_size(axis)
    upper = (lax.axis_index(axis) // bit) % 2 == 1
    first = jnp.logical_not(upper) if forward else upper
    first_state, first_logs = saved
    second_window = jnp.exp(first_logs)[:, None, None] * window + first_state
    keep = jnp.where(first, window, second_window)
    send = jnp.where(first, second_window, window)
    got = lax.ppermute(send, axis, [(j, j ^ bit) for j in range(count)])
    return jnp.where(
        upper, jnp.concatenate([got, keep], axis=0), jnp.concatenate([keep, got], axis=0)
    )


def exclusive_scan(state, logs, axis, forward, extra=None, before_up=None):
    count = lax.axis_size(axis)
    levels = []
    for bit in (1, 2):
        state, logs, saved, extra = pair_down(state, logs, axis, bit, forward, extra)
        levels.append((bit, saved))
    stride = 4
    groups = count // stride
    window_state, window_log = send_with_logs(state, logs, axis, shift_perm(count, stride, forward))
    width = 1
    while width < groups:
        perm = shift_perm(count, stride * width, forward)
        if width * 2 < groups:
            got_state, got_log = send_with_logs(window_state, window_log, axis, perm)
            window_log_next = window_log + got_log
        else:
            got_state = lax.ppermute(window_state, axis, perm)
            window_log_next = window_log
        window_state = window_state + jnp.exp(window_log)[:, None, None] * got_state
        window_log = window_log_next
        width *= 2
    if before_up is not None:
        window_state, done = lax.optimization_barrier((window_state, before_up(extra)))
    for bit, saved in reversed(levels):
        window_state = pair_up(window_state, saved, axis, bit, forward)
    if before_up is not None:
        return window_state, done
    return window_state, extra


def gather_groups(pieces, axis):
    count = lax.axis_size(axis)
    groups = [[z * 4 + r for z in range(count // 4)] for r in range(4)]
    return lax.all_gather(pieces, axis, axis=0, tiled=True, axis_index_groups=groups)


def split_bf16(value):
    upper = lax.reduce_precision(value, exponent_bits=8, mantissa_bits=7)
    return upper.astype(jnp.bfloat16), (value - upper).astype(jnp.bfloat16)


def mp_sum_scatter(value, axis):
    count = lax.axis_size(axis)
    blocks = value.reshape(count, value.shape[0] // count, value.shape[1])
    return jnp.sum(lax.all_to_all(blocks, axis, 0, 0), axis=0)


def attend_kernel(first_ref, query_ref, key_ref, upper_ref, lower_ref, out_ref, top_ref, total_ref, mix_ref, *, heads):
    block = pl.program_id(0)
    rows = query_ref.shape[0]
    width = query_ref.shape[1]
    keys_per_block = key_ref.shape[0]
    first = first_ref[0]

    @pl.when(block == 0)
    def _():
        top_ref[...] = jnp.full(top_ref.shape, very_negative, jnp.float32)
        total_ref[...] = jnp.zeros(total_ref.shape, jnp.float32)
        mix_ref[...] = jnp.zeros(mix_ref.shape, jnp.float32)

    def accumulate(masked):
        scores = lax.dot_general(
            query_ref[...], key_ref[...], (((1,), (1,)), ((), ())), preferred_element_type=jnp.float32
        )
        factor = math.log2(math.e) / math.sqrt(width)
        if masked:
            row = lax.broadcasted_iota(jnp.int32, scores.shape, 0)
            col = lax.broadcasted_iota(jnp.int32, scores.shape, 1)
            allowed = block * keys_per_block + col <= first + row // heads
            scores = jnp.where(allowed, scores, very_negative)
        top_old = top_ref[...]
        top_new = jnp.maximum(top_old, jnp.max(scores, axis=1, keepdims=True))
        rescale = jnp.exp2((top_old - top_new) * factor)
        weights = jnp.exp2((scores - top_new) * factor)
        if masked:
            weights = jnp.where(allowed, weights, 0.0)
        total_ref[...] = rescale * total_ref[...] + jnp.sum(weights, axis=1, keepdims=True)
        weights_hi = weights.astype(jnp.bfloat16)
        weights_lo = (weights - weights_hi.astype(jnp.float32)).astype(jnp.bfloat16)
        upper = upper_ref[...]
        mixed = (
            jnp.dot(weights_hi, upper, preferred_element_type=jnp.float32)
            + jnp.dot(weights_hi, lower_ref[...], preferred_element_type=jnp.float32)
            + jnp.dot(weights_lo, upper, preferred_element_type=jnp.float32)
        )
        mix_ref[...] = rescale * mix_ref[...] + mixed
        top_ref[...] = top_new

    block_end = (block + 1) * keys_per_block - 1

    @pl.when(block_end <= first)
    def _():
        accumulate(False)

    @pl.when(jnp.logical_and(block_end > first, block * keys_per_block <= first + rows // heads - 1))
    def _():
        accumulate(True)

    @pl.when(block == pl.num_programs(0) - 1)
    def _():
        out_ref[...] = mix_ref[...] / total_ref[...]


def attend(first_query, query_rows, every, heads, keys_per_block=512):
    rows, width = query_rows.shape
    blocks = every.shape[0] // keys_per_block
    flops = 2 * rows * every.shape[0] * width * 4
    return pl.pallas_call(
        functools.partial(attend_kernel, heads=heads),
        out_shape=jax.ShapeDtypeStruct((rows, width), jnp.float32),
        grid_spec=pltpu.PrefetchScalarGridSpec(
            num_scalar_prefetch=1,
            grid=(blocks,),
            in_specs=[
                pl.BlockSpec((rows, width), lambda b, f: (0, 0)),
                pl.BlockSpec((keys_per_block, width), lambda b, f: (b, 0)),
                pl.BlockSpec((keys_per_block, width), lambda b, f: (b, 1)),
                pl.BlockSpec((keys_per_block, width), lambda b, f: (b, 2)),
            ],
            out_specs=pl.BlockSpec((rows, width), lambda b, f: (0, 0)),
            scratch_shapes=[
                pltpu.VMEM((rows, 1), jnp.float32),
                pltpu.VMEM((rows, 1), jnp.float32),
                pltpu.VMEM((rows, width), jnp.float32),
            ],
        ),
        compiler_params=pltpu.CompilerParams(dimension_semantics=("arbitrary",)),
        cost_estimate=pl.CostEstimate(
            flops=flops,
            transcendentals=rows * every.shape[0],
            bytes_accessed=every.size * 2 + query_rows.size * 2 + rows * width * 4,
        ),
    )(first_query, query_rows, every, every, every)


def local(queries, keys, values, inputs_x, in_b, in_c, log_decay):
    row_count = queries.shape[0]
    heads = queries.shape[1] // HEAD_WIDTH
    seq_count = lax.axis_size("seq")
    own_index = lax.axis_index("seq")
    first_query = own_index * row_count

    values_hi, values_lo = split_bf16(values)
    packed = jnp.concatenate([keys, values_hi, values_lo], axis=1)

    c_scale = 0.5 / math.sqrt(N * row_count * seq_count)
    student_x = inputs_x.astype(jnp.float32).reshape(row_count, heads, HEAD_WIDTH)
    b_rows = in_b.astype(jnp.float32)
    c_rows = in_c.astype(jnp.float32) * c_scale
    cumulative = jnp.cumsum(log_decay, axis=0)
    totals = cumulative[-1]
    heads_first = cumulative.T
    causal = jnp.arange(row_count)[:, None] >= jnp.arange(row_count)[None, :]
    decays = jnp.exp(
        jnp.where(causal[None], heads_first[:, :, None] - heads_first[:, None, :], -jnp.inf)
    )
    inner_products = jnp.dot(in_c, in_b.T, preferred_element_type=jnp.float32) * c_scale
    mixing = decays * inner_products[None]
    rising = jnp.exp(cumulative)
    ending = jnp.exp(totals[None, :] - cumulative)
    local_state = jnp.einsum(
        "shp,sn->hpn", student_x * ending[:, :, None], b_rows, precision=highest
    )
    query_rows = queries.reshape(row_count * heads, HEAD_WIDTH)

    def teacher(plane_blocks):
        every = gather_groups(plane_blocks, "seq")
        return attend(jnp.reshape(first_query, (1,)).astype(jnp.int32), query_rows, every, heads)

    state_in, teacher_rows = exclusive_scan(local_state, totals, "seq", True, packed, teacher)

    teacher_out = teacher_rows.reshape(row_count, heads, HEAD_WIDTH)

    y_intra = jnp.einsum("hts,shp->thp", mixing, student_x, precision=highest)
    y_inter = jnp.einsum("tn,hpn->thp", c_rows, state_in, precision=highest) * rising[:, :, None]
    mismatch = y_intra + y_inter - teacher_out
    scaled_mismatch = mismatch * rising[:, :, None]
    local_grad = jnp.einsum("thp,tn->hpn", scaled_mismatch, c_rows, precision=highest)
    later_grad, _ = exclusive_scan(local_grad, totals, "seq", False)
    grad_x = jnp.einsum("hts,thp->shp", mixing, mismatch, precision=highest)
    grad_x = (
        grad_x
        + jnp.einsum("hpn,sn->shp", later_grad, b_rows, precision=highest) * ending[:, :, None]
    )
    products = jnp.einsum("thp,shp->hts", mismatch, student_x, precision=highest)
    weighted = decays * products
    grad_b = jnp.einsum("hts,tn->sn", weighted, c_rows, precision=highest)
    grad_b = grad_b + jnp.einsum(
        "shp,hpn->sn", student_x * ending[:, :, None], later_grad, precision=highest
    )
    grad_c = jnp.einsum("hts,sn->tn", weighted, b_rows, precision=highest)
    grad_c = grad_c + jnp.einsum("thp,hpn->tn", scaled_mismatch, state_in, precision=highest)
    summed = mp_sum_scatter(jnp.concatenate([grad_b, grad_c], axis=1), "mp")
    summed_b, summed_c = summed[:, :N], summed[:, N:]
    return (grad_x.reshape(row_count, heads * HEAD_WIDTH), summed_b, summed_c * c_scale)


def solution(mesh):
    in_specs = (
        P("seq", "mp"),
        P("seq", "mp"),
        P("seq", "mp"),
        P("seq", "mp"),
        P("seq", None),
        P("seq", None),
        P("seq", "mp"),
    )
    out_specs = (P("seq", "mp"), P(("seq", "mp"), None), P(("seq", "mp"), None))
    return jax.shard_map(local, mesh=mesh, in_specs=in_specs, out_specs=out_specs, check_vma=False)
```

```python
import functools
import math

import jax
import jax.numpy as jnp
from jax import lax
from jax.experimental import pallas as pl
from jax.experimental.pallas import tpu as pltpu
from jax.sharding import PartitionSpec as P

HEAD_WIDTH = 128
N = 128

very_negative = -1e30
highest = lax.Precision.HIGHEST


def shift(value, axis, distance, forward):
    count = lax.axis_size(axis)
    if forward:
        perm = [(j, j + distance) for j in range(count - distance)]
    else:
        perm = [(j + distance, j) for j in range(count - distance)]
    return lax.ppermute(value, axis, perm)


def send_with_logs(state, logs, axis, perm, extra=None):
    heads, rows, width = state.shape
    count = logs.shape[0]
    log_rows = jnp.pad(jnp.broadcast_to(logs[:, None], (count, width)), ((0, -count % 8), (0, 0)))
    payload = jnp.concatenate([state.reshape(heads * rows, width), log_rows], axis=0)
    if extra is None:
        got = lax.ppermute(payload, axis, perm)
        got_extra = None
    else:
        got, got_extra = lax.ppermute((payload, extra), axis, perm)
    got_state = got[: heads * rows].reshape(heads, rows, width)
    got_logs = got[heads * rows : heads * rows + count, 0]
    if extra is None:
        return got_state, got_logs
    return got_state, got_logs, got_extra


def shift_perm(count, distance, forward):
    if forward:
        return [(j, j + distance) for j in range(count - distance)]
    return [(j + distance, j) for j in range(count - distance)]


def pair_down(state, logs, axis, bit, forward, extra=None):
    count = lax.axis_size(axis)
    upper = (lax.axis_index(axis) // bit) % 2 == 1
    first = jnp.logical_not(upper) if forward else upper
    half = state.shape[0] // 2
    mine = jnp.where(upper, half, 0)
    other = half - mine
    own_state = lax.dynamic_slice_in_dim(state, mine, half, axis=0)
    own_logs = lax.dynamic_slice_in_dim(logs, mine, half)
    sent = send_with_logs(
        lax.dynamic_slice_in_dim(state, other, half, axis=0),
        lax.dynamic_slice_in_dim(logs, other, half),
        axis,
        [(j, j ^ bit) for j in range(count)],
        extra,
    )
    got_state, got_logs = sent[:2]
    joined = None
    if extra is not None:
        joined = sent[2]
        joined = jnp.where(
            upper, jnp.concatenate([joined, extra], axis=0), jnp.concatenate([extra, joined], axis=0)
        )
    first_state = jnp.where(first, own_state, got_state)
    second_state = jnp.where(first, got_state, own_state)
    first_logs = jnp.where(first, own_logs, got_logs)
    second_logs = jnp.where(first, got_logs, own_logs)
    pair_state = jnp.exp(second_logs)[:, None, None] * first_state + second_state
    return pair_state, first_logs + second_logs, (first_state, first_logs), joined


def pair_up(window, saved, axis, bit, forward):
    count = lax.axis_size(axis)
    upper = (lax.axis_index(axis) // bit) % 2 == 1
    first = jnp.logical_not(upper) if forward else upper
    first_state, first_logs = saved
    second_window = jnp.exp(first_logs)[:, None, None] * window + first_state
    keep = jnp.where(first, window, second_window)
    send = jnp.where(first, second_window, window)
    got = lax.ppermute(send, axis, [(j, j ^ bit) for j in range(count)])
    return jnp.where(
        upper, jnp.concatenate([got, keep], axis=0), jnp.concatenate([keep, got], axis=0)
    )


def exclusive_scan(state, logs, axis, forward, extra=None):
    count = lax.axis_size(axis)
    levels = []
    for bit in (1, 2):
        state, logs, saved, extra = pair_down(state, logs, axis, bit, forward, extra)
        levels.append((bit, saved))
    stride = 4
    groups = count // stride
    window_state, window_log = send_with_logs(state, logs, axis, shift_perm(count, stride, forward))
    width = 1
    while width < groups:
        perm = shift_perm(count, stride * width, forward)
        if width * 2 < groups:
            got_state, got_log = send_with_logs(window_state, window_log, axis, perm)
            window_log_next = window_log + got_log
        else:
            got_state = lax.ppermute(window_state, axis, perm)
            window_log_next = window_log
        window_state = window_state + jnp.exp(window_log)[:, None, None] * got_state
        window_log = window_log_next
        width *= 2
    for bit, saved in reversed(levels):
        window_state = pair_up(window_state, saved, axis, bit, forward)
    return window_state, extra


def gather_groups(pieces, axis):
    count = lax.axis_size(axis)
    groups = [[z * 4 + r for z in range(count // 4)] for r in range(4)]
    return lax.all_gather(pieces, axis, axis=0, tiled=True, axis_index_groups=groups)


def split_bf16(value):
    upper = lax.reduce_precision(value, exponent_bits=8, mantissa_bits=7)
    return upper.astype(jnp.bfloat16), (value - upper).astype(jnp.bfloat16)


def mp_sum_scatter(value, axis):
    count = lax.axis_size(axis)
    blocks = value.reshape(count, value.shape[0] // count, value.shape[1])
    return jnp.sum(lax.all_to_all(blocks, axis, 0, 0), axis=0)


def attend_kernel(first_ref, query_ref, key_ref, upper_ref, lower_ref, out_ref, top_ref, total_ref, mix_ref, *, heads):
    block = pl.program_id(0)
    rows = query_ref.shape[0]
    width = query_ref.shape[1]
    keys_per_block = key_ref.shape[0]
    first = first_ref[0]

    @pl.when(block == 0)
    def _():
        top_ref[...] = jnp.full(top_ref.shape, very_negative, jnp.float32)
        total_ref[...] = jnp.zeros(total_ref.shape, jnp.float32)
        mix_ref[...] = jnp.zeros(mix_ref.shape, jnp.float32)

    def accumulate(masked):
        chunk = 128
        factor = math.log2(math.e) / math.sqrt(width)

        def body(step, carry):
            start = pl.multiple_of(step * chunk, chunk)
            rows_now = pl.ds(start, chunk)
            scores = lax.dot_general(
                query_ref[rows_now, :], key_ref[...], (((1,), (1,)), ((), ())),
                preferred_element_type=jnp.float32,
            )
            if masked:
                row = start + lax.broadcasted_iota(jnp.int32, scores.shape, 0)
                col = lax.broadcasted_iota(jnp.int32, scores.shape, 1)
                allowed = block * keys_per_block + col <= first + row // heads
                scores = jnp.where(allowed, scores, very_negative)
            top_old = top_ref[rows_now, :]
            top_new = jnp.maximum(top_old, jnp.max(scores, axis=1, keepdims=True))
            rescale = jnp.exp2((top_old - top_new) * factor)
            weights = jnp.exp2((scores - top_new) * factor)
            if masked:
                weights = jnp.where(allowed, weights, 0.0)
            total_ref[rows_now, :] = rescale * total_ref[rows_now, :] + jnp.sum(weights, axis=1, keepdims=True)
            weights_hi = weights.astype(jnp.bfloat16)
            weights_lo = (weights - weights_hi.astype(jnp.float32)).astype(jnp.bfloat16)
            upper = upper_ref[...]
            mixed = (
                jnp.dot(weights_hi, upper, preferred_element_type=jnp.float32)
                + jnp.dot(weights_hi, lower_ref[...], preferred_element_type=jnp.float32)
                + jnp.dot(weights_lo, upper, preferred_element_type=jnp.float32)
            )
            mix_ref[rows_now, :] = rescale * mix_ref[rows_now, :] + mixed
            top_ref[rows_now, :] = top_new
            return carry

        lax.fori_loop(0, rows // chunk, body, 0)

    block_end = (block + 1) * keys_per_block - 1

    @pl.when(block_end <= first)
    def _():
        accumulate(False)

    @pl.when(jnp.logical_and(block_end > first, block * keys_per_block <= first + rows // heads - 1))
    def _():
        accumulate(True)

    @pl.when(block == pl.num_programs(0) - 1)
    def _():
        out_ref[...] = mix_ref[...] / total_ref[...]


def attend(first_query, query_rows, every, heads, keys_per_block=512):
    rows, width = query_rows.shape
    blocks = every.shape[0] // keys_per_block
    flops = 2 * rows * every.shape[0] * width * 4
    return pl.pallas_call(
        functools.partial(attend_kernel, heads=heads),
        out_shape=jax.ShapeDtypeStruct((rows, width), jnp.float32),
        grid_spec=pltpu.PrefetchScalarGridSpec(
            num_scalar_prefetch=1,
            grid=(blocks,),
            in_specs=[
                pl.BlockSpec((rows, width), lambda b, f: (0, 0)),
                pl.BlockSpec((keys_per_block, width), lambda b, f: (b, 0)),
                pl.BlockSpec((keys_per_block, width), lambda b, f: (b, 1)),
                pl.BlockSpec((keys_per_block, width), lambda b, f: (b, 2)),
            ],
            out_specs=pl.BlockSpec((rows, width), lambda b, f: (0, 0)),
            scratch_shapes=[
                pltpu.VMEM((rows, 1), jnp.float32),
                pltpu.VMEM((rows, 1), jnp.float32),
                pltpu.VMEM((rows, width), jnp.float32),
            ],
        ),
        compiler_params=pltpu.CompilerParams(dimension_semantics=("arbitrary",)),
        cost_estimate=pl.CostEstimate(
            flops=flops,
            transcendentals=rows * every.shape[0],
            bytes_accessed=every.size * 2 + query_rows.size * 2 + rows * width * 4,
        ),
    )(first_query, query_rows, every, every, every)


def local(queries, keys, values, inputs_x, in_b, in_c, log_decay):
    row_count = queries.shape[0]
    heads = queries.shape[1] // HEAD_WIDTH
    seq_count = lax.axis_size("seq")
    own_index = lax.axis_index("seq")
    first_query = own_index * row_count

    values_hi, values_lo = split_bf16(values)
    packed = jnp.concatenate([keys, values_hi, values_lo], axis=1)

    c_scale = 0.5 / math.sqrt(N * row_count * seq_count)
    student_x = inputs_x.astype(jnp.float32).reshape(row_count, heads, HEAD_WIDTH)
    b_rows = in_b.astype(jnp.float32)
    c_rows = in_c.astype(jnp.float32) * c_scale
    cumulative = jnp.cumsum(log_decay, axis=0)
    totals = cumulative[-1]
    heads_first = cumulative.T
    causal = jnp.arange(row_count)[:, None] >= jnp.arange(row_count)[None, :]
    decays = jnp.exp(
        jnp.where(causal[None], heads_first[:, :, None] - heads_first[:, None, :], -jnp.inf)
    )
    inner_products = jnp.dot(in_c, in_b.T, preferred_element_type=jnp.float32) * c_scale
    mixing = decays * inner_products[None]
    rising = jnp.exp(cumulative)
    ending = jnp.exp(totals[None, :] - cumulative)
    local_state = jnp.einsum(
        "shp,sn->hpn", student_x * ending[:, :, None], b_rows, precision=highest
    )
    state_in, plane_blocks = exclusive_scan(local_state, totals, "seq", True, packed)
    every = gather_groups(plane_blocks, "seq")

    query_rows = queries.reshape(row_count * heads, HEAD_WIDTH)
    teacher_out = attend(
        jnp.reshape(first_query, (1,)).astype(jnp.int32), query_rows, every, heads
    ).reshape(row_count, heads, HEAD_WIDTH)

    y_intra = jnp.einsum("hts,shp->thp", mixing, student_x, precision=highest)
    y_inter = jnp.einsum("tn,hpn->thp", c_rows, state_in, precision=highest) * rising[:, :, None]
    mismatch = y_intra + y_inter - teacher_out
    scaled_mismatch = mismatch * rising[:, :, None]
    local_grad = jnp.einsum("thp,tn->hpn", scaled_mismatch, c_rows, precision=highest)
    later_grad, _ = exclusive_scan(local_grad, totals, "seq", False)
    grad_x = jnp.einsum("hts,thp->shp", mixing, mismatch, precision=highest)
    grad_x = (
        grad_x
        + jnp.einsum("hpn,sn->shp", later_grad, b_rows, precision=highest) * ending[:, :, None]
    )
    products = jnp.einsum("thp,shp->hts", mismatch, student_x, precision=highest)
    weighted = decays * products
    grad_b = jnp.einsum("hts,tn->sn", weighted, c_rows, precision=highest)
    grad_b = grad_b + jnp.einsum(
        "shp,hpn->sn", student_x * ending[:, :, None], later_grad, precision=highest
    )
    grad_c = jnp.einsum("hts,sn->tn", weighted, b_rows, precision=highest)
    grad_c = grad_c + jnp.einsum("thp,hpn->tn", scaled_mismatch, state_in, precision=highest)
    summed = mp_sum_scatter(jnp.concatenate([grad_b, grad_c], axis=1), "mp")
    summed_b, summed_c = summed[:, :N], summed[:, N:]
    return (grad_x.reshape(row_count, heads * HEAD_WIDTH), summed_b, summed_c * c_scale)


def solution(mesh):
    in_specs = (
        P("seq", "mp"),
        P("seq", "mp"),
        P("seq", "mp"),
        P("seq", "mp"),
        P("seq", None),
        P("seq", None),
        P("seq", "mp"),
    )
    out_specs = (P("seq", "mp"), P(("seq", "mp"), None), P(("seq", "mp"), None))
    return jax.shard_map(local, mesh=mesh, in_specs=in_specs, out_specs=out_specs, check_vma=False)
```

```python
import functools
import math

import jax
import jax.numpy as jnp
from jax import lax
from jax.experimental import pallas as pl
from jax.experimental.pallas import tpu as pltpu
from jax.sharding import PartitionSpec as P

HEAD_WIDTH = 128
N = 128

very_negative = -1e30
highest = lax.Precision.HIGHEST


def shift(value, axis, distance, forward):
    count = lax.axis_size(axis)
    if forward:
        perm = [(j, j + distance) for j in range(count - distance)]
    else:
        perm = [(j + distance, j) for j in range(count - distance)]
    return lax.ppermute(value, axis, perm)


def send_with_logs(state, logs, axis, perm, extra=None):
    heads, rows, width = state.shape
    count = logs.shape[0]
    log_rows = jnp.pad(jnp.broadcast_to(logs[:, None], (count, width)), ((0, -count % 8), (0, 0)))
    payload = jnp.concatenate([state.reshape(heads * rows, width), log_rows], axis=0)
    if extra is None:
        got = lax.ppermute(payload, axis, perm)
        got_extra = None
    else:
        got, got_extra = lax.ppermute((payload, extra), axis, perm)
    got_state = got[: heads * rows].reshape(heads, rows, width)
    got_logs = got[heads * rows : heads * rows + count, 0]
    if extra is None:
        return got_state, got_logs
    return got_state, got_logs, got_extra


def shift_perm(count, distance, forward):
    if forward:
        return [(j, j + distance) for j in range(count - distance)]
    return [(j + distance, j) for j in range(count - distance)]


def pair_down(state, logs, axis, bit, forward, extra=None):
    count = lax.axis_size(axis)
    upper = (lax.axis_index(axis) // bit) % 2 == 1
    first = jnp.logical_not(upper) if forward else upper
    half = state.shape[0] // 2
    mine = jnp.where(upper, half, 0)
    other = half - mine
    own_state = lax.dynamic_slice_in_dim(state, mine, half, axis=0)
    own_logs = lax.dynamic_slice_in_dim(logs, mine, half)
    sent = send_with_logs(
        lax.dynamic_slice_in_dim(state, other, half, axis=0),
        lax.dynamic_slice_in_dim(logs, other, half),
        axis,
        [(j, j ^ bit) for j in range(count)],
        extra,
    )
    got_state, got_logs = sent[:2]
    joined = None
    if extra is not None:
        joined = sent[2]
        joined = jnp.where(
            upper, jnp.concatenate([joined, extra], axis=0), jnp.concatenate([extra, joined], axis=0)
        )
    first_state = jnp.where(first, own_state, got_state)
    second_state = jnp.where(first, got_state, own_state)
    first_logs = jnp.where(first, own_logs, got_logs)
    second_logs = jnp.where(first, got_logs, own_logs)
    pair_state = jnp.exp(second_logs)[:, None, None] * first_state + second_state
    return pair_state, first_logs + second_logs, (first_state, first_logs), joined


def pair_up(window, saved, axis, bit, forward):
    count = lax.axis_size(axis)
    upper = (lax.axis_index(axis) // bit) % 2 == 1
    first = jnp.logical_not(upper) if forward else upper
    first_state, first_logs = saved
    second_window = jnp.exp(first_logs)[:, None, None] * window + first_state
    keep = jnp.where(first, window, second_window)
    send = jnp.where(first, second_window, window)
    got = lax.ppermute(send, axis, [(j, j ^ bit) for j in range(count)])
    return jnp.where(
        upper, jnp.concatenate([got, keep], axis=0), jnp.concatenate([keep, got], axis=0)
    )


def exclusive_scan(state, logs, axis, forward, extra=None):
    count = lax.axis_size(axis)
    levels = []
    for bit in (1, 2):
        state, logs, saved, extra = pair_down(state, logs, axis, bit, forward, extra)
        levels.append((bit, saved))
    stride = 4
    groups = count // stride
    window_state, window_log = send_with_logs(state, logs, axis, shift_perm(count, stride, forward))
    width = 1
    while width < groups:
        perm = shift_perm(count, stride * width, forward)
        if width * 2 < groups:
            got_state, got_log = send_with_logs(window_state, window_log, axis, perm)
            window_log_next = window_log + got_log
        else:
            got_state = lax.ppermute(window_state, axis, perm)
            window_log_next = window_log
        window_state = window_state + jnp.exp(window_log)[:, None, None] * got_state
        window_log = window_log_next
        width *= 2
    for bit, saved in reversed(levels):
        window_state = pair_up(window_state, saved, axis, bit, forward)
    return window_state, extra


def gather_groups(pieces, axis):
    count = lax.axis_size(axis)
    groups = [[z * 4 + r for z in range(count // 4)] for r in range(4)]
    return lax.all_gather(pieces, axis, axis=0, tiled=True, axis_index_groups=groups)


def split_bf16(value):
    upper = lax.reduce_precision(value, exponent_bits=8, mantissa_bits=7)
    return upper.astype(jnp.bfloat16), (value - upper).astype(jnp.bfloat16)


def mp_sum_scatter(value, axis):
    count = lax.axis_size(axis)
    blocks = value.reshape(count, value.shape[0] // count, value.shape[1])
    return jnp.sum(lax.all_to_all(blocks, axis, 0, 0), axis=0)


def attend_kernel(first_ref, query_ref, key_ref, upper_ref, lower_ref, out_ref, top_ref, total_ref, mix_ref, *, heads):
    block = pl.program_id(0)
    rows = query_ref.shape[0]
    width = query_ref.shape[1]
    keys_per_block = key_ref.shape[0]
    first = first_ref[0]

    @pl.when(block == 0)
    def _():
        top_ref[...] = jnp.full(top_ref.shape, very_negative, jnp.float32)
        total_ref[...] = jnp.zeros(total_ref.shape, jnp.float32)
        mix_ref[...] = jnp.zeros(mix_ref.shape, jnp.float32)

    def accumulate(masked):
        scores = lax.dot_general(
            query_ref[...], key_ref[...], (((1,), (1,)), ((), ())), preferred_element_type=jnp.float32
        )
        factor = math.log2(math.e) / math.sqrt(width)
        if masked:
            row = lax.broadcasted_iota(jnp.int32, scores.shape, 0)
            col = lax.broadcasted_iota(jnp.int32, scores.shape, 1)
            allowed = block * keys_per_block + col <= first + row // heads
            scores = jnp.where(allowed, scores, very_negative)
        top_old = top_ref[...]
        top_new = jnp.maximum(top_old, jnp.max(scores, axis=1, keepdims=True))
        rescale = jnp.exp2((top_old - top_new) * factor)
        weights = jnp.exp2((scores - top_new) * factor)
        if masked:
            weights = jnp.where(allowed, weights, 0.0)
        total_ref[...] = rescale * total_ref[...] + jnp.sum(weights, axis=1, keepdims=True)
        weights_hi = weights.astype(jnp.bfloat16)
        weights_lo = (weights - weights_hi.astype(jnp.float32)).astype(jnp.bfloat16)
        upper = upper_ref[...]
        mixed = (
            jnp.dot(weights_hi, upper, preferred_element_type=jnp.float32)
            + jnp.dot(weights_hi, lower_ref[...], preferred_element_type=jnp.float32)
            + jnp.dot(weights_lo, upper, preferred_element_type=jnp.float32)
        )
        mix_ref[...] = rescale * mix_ref[...] + mixed
        top_ref[...] = top_new

    block_end = (block + 1) * keys_per_block - 1

    @pl.when(block_end <= first)
    def _():
        accumulate(False)

    @pl.when(jnp.logical_and(block_end > first, block * keys_per_block <= first + rows // heads - 1))
    def _():
        accumulate(True)

    @pl.when(block == pl.num_programs(0) - 1)
    def _():
        out_ref[...] = mix_ref[...] / total_ref[...]


def attend(first_query, query_rows, every, heads, keys_per_block=256):
    rows, width = query_rows.shape
    blocks = every.shape[0] // keys_per_block
    flops = 2 * rows * every.shape[0] * width * 4
    return pl.pallas_call(
        functools.partial(attend_kernel, heads=heads),
        out_shape=jax.ShapeDtypeStruct((rows, width), jnp.float32),
        grid_spec=pltpu.PrefetchScalarGridSpec(
            num_scalar_prefetch=1,
            grid=(blocks,),
            in_specs=[
                pl.BlockSpec((rows, width), lambda b, f: (0, 0)),
                pl.BlockSpec((keys_per_block, width), lambda b, f: (b, 0)),
                pl.BlockSpec((keys_per_block, width), lambda b, f: (b, 1)),
                pl.BlockSpec((keys_per_block, width), lambda b, f: (b, 2)),
            ],
            out_specs=pl.BlockSpec((rows, width), lambda b, f: (0, 0)),
            scratch_shapes=[
                pltpu.VMEM((rows, 1), jnp.float32),
                pltpu.VMEM((rows, 1), jnp.float32),
                pltpu.VMEM((rows, width), jnp.float32),
            ],
        ),
        compiler_params=pltpu.CompilerParams(dimension_semantics=("arbitrary",)),
        cost_estimate=pl.CostEstimate(
            flops=flops,
            transcendentals=rows * every.shape[0],
            bytes_accessed=every.size * 2 + query_rows.size * 2 + rows * width * 4,
        ),
    )(first_query, query_rows, every, every, every)


def local(queries, keys, values, inputs_x, in_b, in_c, log_decay):
    row_count = queries.shape[0]
    heads = queries.shape[1] // HEAD_WIDTH
    seq_count = lax.axis_size("seq")
    own_index = lax.axis_index("seq")
    first_query = own_index * row_count

    values_hi, values_lo = split_bf16(values)
    packed = jnp.concatenate([keys, values_hi, values_lo], axis=1)

    c_scale = 0.5 / math.sqrt(N * row_count * seq_count)
    student_x = inputs_x.astype(jnp.float32).reshape(row_count, heads, HEAD_WIDTH)
    b_rows = in_b.astype(jnp.float32)
    c_rows = in_c.astype(jnp.float32) * c_scale
    cumulative = jnp.cumsum(log_decay, axis=0)
    totals = cumulative[-1]
    heads_first = cumulative.T
    causal = jnp.arange(row_count)[:, None] >= jnp.arange(row_count)[None, :]
    decays = jnp.exp(
        jnp.where(causal[None], heads_first[:, :, None] - heads_first[:, None, :], -jnp.inf)
    )
    inner_products = jnp.dot(in_c, in_b.T, preferred_element_type=jnp.float32) * c_scale
    mixing = decays * inner_products[None]
    rising = jnp.exp(cumulative)
    ending = jnp.exp(totals[None, :] - cumulative)
    local_state = jnp.einsum(
        "shp,sn->hpn", student_x * ending[:, :, None], b_rows, precision=highest
    )
    state_in, plane_blocks = exclusive_scan(local_state, totals, "seq", True, packed)
    every = gather_groups(plane_blocks, "seq")

    query_rows = queries.reshape(row_count * heads, HEAD_WIDTH)
    teacher_out = attend(
        jnp.reshape(first_query, (1,)).astype(jnp.int32), query_rows, every, heads
    ).reshape(row_count, heads, HEAD_WIDTH)

    y_intra = jnp.einsum("hts,shp->thp", mixing, student_x, precision=highest)
    y_inter = jnp.einsum("tn,hpn->thp", c_rows, state_in, precision=highest) * rising[:, :, None]
    mismatch = y_intra + y_inter - teacher_out
    scaled_mismatch = mismatch * rising[:, :, None]
    local_grad = jnp.einsum("thp,tn->hpn", scaled_mismatch, c_rows, precision=highest)
    later_grad, _ = exclusive_scan(local_grad, totals, "seq", False)
    grad_x = jnp.einsum("hts,thp->shp", mixing, mismatch, precision=highest)
    grad_x = (
        grad_x
        + jnp.einsum("hpn,sn->shp", later_grad, b_rows, precision=highest) * ending[:, :, None]
    )
    products = jnp.einsum("thp,shp->hts", mismatch, student_x, precision=highest)
    weighted = decays * products
    grad_b = jnp.einsum("hts,tn->sn", weighted, c_rows, precision=highest)
    grad_b = grad_b + jnp.einsum(
        "shp,hpn->sn", student_x * ending[:, :, None], later_grad, precision=highest
    )
    grad_c = jnp.einsum("hts,sn->tn", weighted, b_rows, precision=highest)
    grad_c = grad_c + jnp.einsum("thp,hpn->tn", scaled_mismatch, state_in, precision=highest)
    summed = mp_sum_scatter(jnp.concatenate([grad_b, grad_c], axis=1), "mp")
    summed_b, summed_c = summed[:, :N], summed[:, N:]
    return (grad_x.reshape(row_count, heads * HEAD_WIDTH), summed_b, summed_c * c_scale)


def solution(mesh):
    in_specs = (
        P("seq", "mp"),
        P("seq", "mp"),
        P("seq", "mp"),
        P("seq", "mp"),
        P("seq", None),
        P("seq", None),
        P("seq", "mp"),
    )
    out_specs = (P("seq", "mp"), P(("seq", "mp"), None), P(("seq", "mp"), None))
    return jax.shard_map(local, mesh=mesh, in_specs=in_specs, out_specs=out_specs, check_vma=False)
```

```python
import functools
import math

import jax
import jax.numpy as jnp
from jax import lax
from jax.experimental import pallas as pl
from jax.experimental.pallas import tpu as pltpu
from jax.sharding import PartitionSpec as P

HEAD_WIDTH = 128
N = 128

very_negative = -1e30
highest = lax.Precision.HIGHEST


def shift(value, axis, distance, forward):
    count = lax.axis_size(axis)
    if forward:
        perm = [(j, j + distance) for j in range(count - distance)]
    else:
        perm = [(j + distance, j) for j in range(count - distance)]
    return lax.ppermute(value, axis, perm)


def send_with_logs(state, logs, axis, perm, extra=None):
    heads, rows, width = state.shape
    count = logs.shape[0]
    log_rows = jnp.pad(jnp.broadcast_to(logs[:, None], (count, width)), ((0, -count % 8), (0, 0)))
    payload = jnp.concatenate([state.reshape(heads * rows, width), log_rows], axis=0)
    if extra is None:
        got = lax.ppermute(payload, axis, perm)
        got_extra = None
    else:
        got, got_extra = lax.ppermute((payload, extra), axis, perm)
    got_state = got[: heads * rows].reshape(heads, rows, width)
    got_logs = got[heads * rows : heads * rows + count, 0]
    if extra is None:
        return got_state, got_logs
    return got_state, got_logs, got_extra


def shift_perm(count, distance, forward):
    if forward:
        return [(j, j + distance) for j in range(count - distance)]
    return [(j + distance, j) for j in range(count - distance)]


def pair_down(state, logs, axis, bit, forward, extra=None):
    count = lax.axis_size(axis)
    upper = (lax.axis_index(axis) // bit) % 2 == 1
    first = jnp.logical_not(upper) if forward else upper
    half = state.shape[0] // 2
    mine = jnp.where(upper, half, 0)
    other = half - mine
    own_state = lax.dynamic_slice_in_dim(state, mine, half, axis=0)
    own_logs = lax.dynamic_slice_in_dim(logs, mine, half)
    sent = send_with_logs(
        lax.dynamic_slice_in_dim(state, other, half, axis=0),
        lax.dynamic_slice_in_dim(logs, other, half),
        axis,
        [(j, j ^ bit) for j in range(count)],
        extra,
    )
    got_state, got_logs = sent[:2]
    joined = None
    if extra is not None:
        joined = sent[2]
        joined = jnp.where(
            upper, jnp.concatenate([joined, extra], axis=0), jnp.concatenate([extra, joined], axis=0)
        )
    first_state = jnp.where(first, own_state, got_state)
    second_state = jnp.where(first, got_state, own_state)
    first_logs = jnp.where(first, own_logs, got_logs)
    second_logs = jnp.where(first, got_logs, own_logs)
    pair_state = jnp.exp(second_logs)[:, None, None] * first_state + second_state
    return pair_state, first_logs + second_logs, (first_state, first_logs), joined


def pair_up(window, saved, axis, bit, forward):
    count = lax.axis_size(axis)
    upper = (lax.axis_index(axis) // bit) % 2 == 1
    first = jnp.logical_not(upper) if forward else upper
    first_state, first_logs = saved
    second_window = jnp.exp(first_logs)[:, None, None] * window + first_state
    keep = jnp.where(first, window, second_window)
    send = jnp.where(first, second_window, window)
    got = lax.ppermute(send, axis, [(j, j ^ bit) for j in range(count)])
    return jnp.where(
        upper, jnp.concatenate([got, keep], axis=0), jnp.concatenate([keep, got], axis=0)
    )


def exclusive_scan(state, logs, axis, forward, extra=None):
    count = lax.axis_size(axis)
    levels = []
    for bit in (1, 2):
        state, logs, saved, extra = pair_down(state, logs, axis, bit, forward, extra)
        levels.append((bit, saved))
    stride = 4
    groups = count // stride
    window_state, window_log = send_with_logs(state, logs, axis, shift_perm(count, stride, forward))
    width = 1
    while width < groups:
        perm = shift_perm(count, stride * width, forward)
        if width * 2 < groups:
            got_state, got_log = send_with_logs(window_state, window_log, axis, perm)
            window_log_next = window_log + got_log
        else:
            got_state = lax.ppermute(window_state, axis, perm)
            window_log_next = window_log
        window_state = window_state + jnp.exp(window_log)[:, None, None] * got_state
        window_log = window_log_next
        width *= 2
    for bit, saved in reversed(levels):
        window_state = pair_up(window_state, saved, axis, bit, forward)
    return window_state, extra


def gather_groups(pieces, axis):
    count = lax.axis_size(axis)
    groups = [[z * 4 + r for z in range(count // 4)] for r in range(4)]
    return lax.all_gather(pieces, axis, axis=0, tiled=True, axis_index_groups=groups)


def split_bf16(value):
    upper = lax.reduce_precision(value, exponent_bits=8, mantissa_bits=7)
    return upper.astype(jnp.bfloat16), (value - upper).astype(jnp.bfloat16)


def mp_sum_scatter(value, axis):
    count = lax.axis_size(axis)
    blocks = value.reshape(count, value.shape[0] // count, value.shape[1])
    return jnp.sum(lax.all_to_all(blocks, axis, 0, 0), axis=0)


def attend_kernel(first_ref, query_ref, key_ref, upper_ref, lower_ref, out_ref, top_ref, total_ref, mix_ref, *, heads):
    block = pl.program_id(0)
    rows = query_ref.shape[0]
    width = query_ref.shape[1]
    keys_per_block = key_ref.shape[0]
    first = first_ref[0]

    @pl.when(block == 0)
    def _():
        top_ref[...] = jnp.full(top_ref.shape, very_negative, jnp.float32)
        total_ref[...] = jnp.zeros(total_ref.shape, jnp.float32)
        mix_ref[...] = jnp.zeros(mix_ref.shape, jnp.float32)

    def accumulate(masked):
        scores = lax.dot_general(
            query_ref[...], key_ref[...], (((1,), (1,)), ((), ())), preferred_element_type=jnp.float32
        )
        factor = math.log2(math.e) / math.sqrt(width)
        if masked:
            row = lax.broadcasted_iota(jnp.int32, scores.shape, 0)
            col = lax.broadcasted_iota(jnp.int32, scores.shape, 1)
            allowed = block * keys_per_block + col <= first + row // heads
            scores = jnp.where(allowed, scores, very_negative)
        top_old = top_ref[...]
        top_new = jnp.maximum(top_old, jnp.max(scores, axis=1, keepdims=True))
        rescale = jnp.exp2((top_old - top_new) * factor)
        weights = jnp.exp2((scores - top_new) * factor)
        if masked:
            weights = jnp.where(allowed, weights, 0.0)
        total_ref[...] = rescale * total_ref[...] + jnp.sum(weights, axis=1, keepdims=True)
        weights_hi = weights.astype(jnp.bfloat16)
        weights_lo = (weights - weights_hi.astype(jnp.float32)).astype(jnp.bfloat16)
        upper = upper_ref[...]
        mixed = (
            jnp.dot(weights_hi, upper, preferred_element_type=jnp.float32)
            + jnp.dot(weights_hi, lower_ref[...], preferred_element_type=jnp.float32)
            + jnp.dot(weights_lo, upper, preferred_element_type=jnp.float32)
        )
        mix_ref[...] = rescale * mix_ref[...] + mixed
        top_ref[...] = top_new

    block_end = (block + 1) * keys_per_block - 1

    @pl.when(block_end <= first)
    def _():
        accumulate(False)

    @pl.when(jnp.logical_and(block_end > first, block * keys_per_block <= first + rows // heads - 1))
    def _():
        accumulate(True)

    @pl.when(block == pl.num_programs(0) - 1)
    def _():
        out_ref[...] = mix_ref[...] / total_ref[...]


def attend(first_query, query_rows, every, heads, keys_per_block=512):
    rows, width = query_rows.shape
    blocks = every.shape[0] // keys_per_block
    flops = 2 * rows * every.shape[0] * width * 4
    return pl.pallas_call(
        functools.partial(attend_kernel, heads=heads),
        out_shape=jax.ShapeDtypeStruct((rows, width), jnp.float32),
        grid_spec=pltpu.PrefetchScalarGridSpec(
            num_scalar_prefetch=1,
            grid=(blocks,),
            in_specs=[
                pl.BlockSpec((rows, width), lambda b, f: (0, 0)),
                pl.BlockSpec((keys_per_block, width), lambda b, f: (b, 0)),
                pl.BlockSpec((keys_per_block, width), lambda b, f: (b, 1)),
                pl.BlockSpec((keys_per_block, width), lambda b, f: (b, 2)),
            ],
            out_specs=pl.BlockSpec((rows, width), lambda b, f: (0, 0)),
            scratch_shapes=[
                pltpu.VMEM((rows, 1), jnp.float32),
                pltpu.VMEM((rows, 1), jnp.float32),
                pltpu.VMEM((rows, width), jnp.float32),
            ],
        ),
        compiler_params=pltpu.CompilerParams(dimension_semantics=("arbitrary",)),
        cost_estimate=pl.CostEstimate(
            flops=flops,
            transcendentals=rows * every.shape[0],
            bytes_accessed=every.size * 2 + query_rows.size * 2 + rows * width * 4,
        ),
    )(first_query, query_rows, every, every, every)


def local(queries, keys, values, inputs_x, in_b, in_c, log_decay):
    row_count = queries.shape[0]
    heads = queries.shape[1] // HEAD_WIDTH
    seq_count = lax.axis_size("seq")
    own_index = lax.axis_index("seq")
    first_query = own_index * row_count

    values_hi, values_lo = split_bf16(values)
    packed = jnp.concatenate([keys, values_hi, values_lo], axis=1)

    c_scale = 0.5 / math.sqrt(N * row_count * seq_count)
    student_x = inputs_x.astype(jnp.float32).reshape(row_count, heads, HEAD_WIDTH)
    b_rows = in_b.astype(jnp.float32)
    c_rows = in_c.astype(jnp.float32) * c_scale
    cumulative = jnp.cumsum(log_decay, axis=0)
    totals = cumulative[-1]
    heads_first = cumulative.T
    causal = jnp.arange(row_count)[:, None] >= jnp.arange(row_count)[None, :]
    decays = jnp.exp(
        jnp.where(causal[None], heads_first[:, :, None] - heads_first[:, None, :], -jnp.inf)
    )
    inner_products = jnp.dot(in_c, in_b.T, preferred_element_type=jnp.float32) * c_scale
    mixing = decays * inner_products[None]
    rising = jnp.exp(cumulative)
    ending = jnp.exp(totals[None, :] - cumulative)
    local_state = jnp.einsum(
        "shp,sn->hpn", student_x * ending[:, :, None], b_rows, precision=highest
    )
    state_in, plane_blocks = exclusive_scan(local_state, totals, "seq", True, packed)
    every = gather_groups(plane_blocks, "seq")

    query_rows = queries.reshape(row_count * heads, HEAD_WIDTH)
    teacher_out = attend(
        jnp.reshape(first_query, (1,)).astype(jnp.int32), query_rows, every, heads
    ).reshape(row_count, heads, HEAD_WIDTH)

    y_intra = jnp.einsum("hts,shp->thp", mixing, student_x, precision=highest)
    y_inter = jnp.einsum("tn,hpn->thp", c_rows, state_in, precision=highest) * rising[:, :, None]
    mismatch = y_intra + y_inter - teacher_out
    scaled_mismatch = mismatch * rising[:, :, None]
    local_grad = jnp.einsum("thp,tn->hpn", scaled_mismatch, c_rows, precision=highest)
    later_grad, _ = exclusive_scan(local_grad, totals, "seq", False)
    grad_x = jnp.einsum("hts,thp->shp", mixing, mismatch, precision=highest)
    grad_x = (
        grad_x
        + jnp.einsum("hpn,sn->shp", later_grad, b_rows, precision=highest) * ending[:, :, None]
    )
    products = jnp.einsum("thp,shp->hts", mismatch, student_x, precision=highest)
    weighted = decays * products
    grad_b = jnp.einsum("hts,tn->sn", weighted, c_rows, precision=highest)
    grad_b = grad_b + jnp.einsum(
        "shp,hpn->sn", student_x * ending[:, :, None], later_grad, precision=highest
    )
    grad_c = jnp.einsum("hts,sn->tn", weighted, b_rows, precision=highest)
    grad_c = grad_c + jnp.einsum("thp,hpn->tn", scaled_mismatch, state_in, precision=highest)
    summed = mp_sum_scatter(jnp.concatenate([grad_b, grad_c * c_scale], axis=1), "mp")
    summed_b, summed_c = summed[:, :N], summed[:, N:]
    return (grad_x.reshape(row_count, heads * HEAD_WIDTH), summed_b, summed_c)


def solution(mesh):
    in_specs = (
        P("seq", "mp"),
        P("seq", "mp"),
        P("seq", "mp"),
        P("seq", "mp"),
        P("seq", None),
        P("seq", None),
        P("seq", "mp"),
    )
    out_specs = (P("seq", "mp"), P(("seq", "mp"), None), P(("seq", "mp"), None))
    return jax.shard_map(local, mesh=mesh, in_specs=in_specs, out_specs=out_specs, check_vma=False)
```
